512 devices in a mesh: tensor: 32 (over z_hi, x, core), seq: 16 (over z_lo, y).
Axes of the slice: x: 4, y: 4, z: 16 (z_hi: 4, z_lo: 4; z = z_hi * 4 + z_lo), core: 2. Of those that a mesh axis runs over, the one named last changes fastest.
Arguments:
- resid: bfloat16 [16, 512, 2048], P('seq', 'tensor'), may hold values from -6 to 6
- norm_gain: bfloat16 [2048], replicated, may hold values from 0.099609375 to 1.8984375
- gate_weight_matrix: bfloat16 [2048, 10944], P(None, 'tensor'), may hold values from -0.125 to 0.125
- up_weight: bfloat16 [2048, 10944], P(None, 'tensor'), may hold values from -0.125 to 0.125
- w_down: bfloat16 [10944, 2048], P('tensor'), may hold values from -0.0546875 to 0.0546875
- gate_a: bfloat16 [64, 2048, 16], P('seq', 'tensor'), may hold values from -0.125 to 0.125
- gate_b: bfloat16 [64, 16, 10944], P('seq', None, 'tensor'), may hold values from -1.5 to 1.5
- up_a: bfloat16 [64, 2048, 16], P('seq', 'tensor'), may hold values from -0.125 to 0.125
- up_b: bfloat16 [64, 16, 10944], P('seq', None, 'tensor'), may hold values from -1.5 to 1.5
- down_a: bfloat16 [64, 10944, 16], P('seq', 'tensor'), may hold values from -0.0546875 to 0.0546875
- down_b: bfloat16 [64, 16, 2048], P('seq'), may hold values from -1.5 to 1.5
- prompt_lengths: int32 [16, 8], P('seq'), may hold values from 1 to 256, 512 in all within a row
- prompt_choice: int32 [16, 8], P('seq'), may hold values from 0 to 15
- used_adapters: int32 [16], replicated, may hold values from 0 to 63, as said below
- adapter_holder: int32 [64], replicated, may hold values from 0 to 63, each once
Outputs:
- output: bfloat16 [16, 512, 2048], P('seq', 'tensor')
The draws below stay inside these ranges and needn't reach their ends.
Inputs may be any that keep to these rules, and one draw needn't show every extreme that they name: `used_adapters`: 16 distinct adapter ids.
All inputs are finite; a program needn't handle non-finite values.
Results may differ from the reference program's by a relative error of at most 0.017.
Values may be sent and summed in bfloat16 or wider, within the bound.
No kernel may reach another device: no remote copies, remote signals or barrier semaphores. Data moves between devices by JAX's collectives and lax.ppermute only.
A program may use at most 128 MiB of HBM per device.

```python
import math
import jax
import jax.numpy as jnp
import numpy as np
from jax import lax

D = 2048
FF = 10944
RANK = 16
USED = 16
PROMPTS = 8
GROUP_TOK = 512
LONGEST = 256
GROUPS = 16
ADAPTERS = 64
N_TENSOR = 32


def draw_used_adapters(key, part):
    first_key = jax.random.fold_in(key, 11)
    second_key = jax.random.fold_in(key, 12)
    middle = 1 + jax.random.permutation(first_key, ADAPTERS - 2)[:USED - 2]
    corners = jnp.array([0, ADAPTERS - 1], jnp.int32)
    whole = jnp.concatenate([corners, middle.astype(jnp.int32)])
    order = jax.random.permutation(second_key, USED)
    return whole[order]


def touch_ends(values, stream_key, least, largest):
    longest = values.shape.index(max(values.shape))
    spots = []
    for shift in (0, 1):
        where = [jax.random.randint(jax.random.fold_in(stream_key, axis), (), 0, length) for axis, length in enumerate(values.shape)]
        where[longest] = (where[longest] + shift) % values.shape[longest]
        spots.append(tuple(where))
    return values.at[spots[0]].set(least).at[spots[1]].set(largest)


def block_levels(stream_key, shape, shards, low, top_value):
    def one(position, parts):
        steps = jax.random.uniform(jax.random.fold_in(jax.random.fold_in(stream_key, 6), position), (parts,), jnp.float32, low / len(shards), top_value / len(shards))
        return jnp.repeat(jnp.exp(steps), shape[position] // parts).reshape((-1,) + (1,) * (len(shape) - position - 1))

    gain = one(*shards[0])
    for cut in shards[1:]:
        gain = gain * one(*cut)
    return gain


def length_profile(number_of, total, reach, skew):
    loads = [(1 << 20) // math.isqrt(grade ** skew) + 1 for grade in range(2, number_of + 1)]
    surplus, given = total - reach - (number_of - 1), [1] * (number_of - 1)
    while surplus > 0:
        candidates = [i for i in range(number_of - 1) if given[i] < reach]
        pool, left = sum([loads[i] for i in candidates]), surplus
        for i in candidates:
            more = min(reach - given[i], max(1, left * loads[i] // pool), surplus)
            given[i] = given[i] + more
            surplus = surplus - more
    return np.array([reach] + given)


def ragged_sizes(own_key, amount, total, bound, lean):
    if amount == 2:
        one = jax.random.randint(own_key, (), max(1, total - bound), min(bound, total - 1) + 1)
        return jnp.stack([one, total - one])
    sizes = jnp.asarray(length_profile(amount, total, bound, lean), jnp.int32)
    pairs = (amount - 1) // 2
    giver, receiver = sizes[1:1 + 2 * pairs:2], sizes[2:2 + 2 * pairs:2]
    room = jnp.minimum(giver - 1, bound - receiver)
    passed = jax.random.randint(jax.random.fold_in(own_key, 1), (pairs,), 0, 1 << 20) % (room + 1)
    sizes = sizes.at[1:1 + 2 * pairs:2].set(giver - passed).at[2:2 + 2 * pairs:2].set(receiver + passed)
    return sizes[jax.random.permutation(jax.random.fold_in(own_key, 2), amount)]


def normal_values(rng, extent, width, bound, pieces=(), kind=jnp.bfloat16):
    factor_of = block_levels(rng, extent, pieces, -0.22, 0.18) if pieces else 1.0
    values = jax.random.normal(rng, extent, jnp.float32) * width * factor_of
    return jnp.minimum(jnp.maximum(values, -bound), bound).astype(kind)


def setup_inputs(seed: int = 0) -> dict:
    arg_keys = jax.random.split(jax.random.key(seed), 16)
    return {
        "resid": normal_values(arg_keys[0], (GROUPS, GROUP_TOK, D), 1.0, 6.0, ((0, 16), (1, 32))),
        "norm_gain": jnp.clip(1.0 + 0.18 * jax.random.normal(arg_keys[1], (D,), jnp.float32), 0.099609375, 1.8984375).astype(jnp.bfloat16),
        "gate_weight_matrix": normal_values(arg_keys[2], (D, FF), D ** -0.5, 0.125, ((1, 32),)),
        "up_weight": normal_values(arg_keys[3], (D, FF), D ** -0.5, 0.125, ((1, 32),)),
        "w_down": normal_values(arg_keys[4], (FF, D), FF ** -0.5, 0.0546875, ((0, 32),)),
        "gate_a": normal_values(arg_keys[5], (ADAPTERS, D, RANK), D ** -0.5, 0.125, ((0, 16), (1, 32))),
        "gate_b": normal_values(arg_keys[6], (ADAPTERS, RANK, FF), RANK ** -0.5, 1.5, ((0, 16), (2, 32))),
        "up_a": normal_values(arg_keys[7], (ADAPTERS, D, RANK), D ** -0.5, 0.125, ((0, 16), (1, 32))),
        "up_b": normal_values(arg_keys[8], (ADAPTERS, RANK, FF), RANK ** -0.5, 1.5, ((0, 16), (2, 32))),
        "down_a": normal_values(arg_keys[9], (ADAPTERS, FF, RANK), FF ** -0.5, 0.0546875, ((0, 16), (1, 32))),
        "down_b": normal_values(arg_keys[10], (ADAPTERS, RANK, D), RANK ** -0.5, 1.5, ((0, 16),)),
        "prompt_lengths": jax.vmap(lambda own: ragged_sizes(own, PROMPTS, GROUP_TOK, LONGEST, 2))(jax.random.split(arg_keys[11], GROUPS)).reshape((GROUPS, PROMPTS)).astype(jnp.int32),
        "prompt_choice": touch_ends(jax.random.randint(arg_keys[12], (GROUPS, PROMPTS), 0, USED), jax.random.fold_in(arg_keys[12], 1), 0, USED - 1).astype(jnp.int32),
        "used_adapters": draw_used_adapters(jax.random.fold_in(arg_keys[15], 71), 0),
        "adapter_holder": jax.random.permutation(arg_keys[14], ADAPTERS).astype(jnp.int32),
    }


adapter_scale = 0.5

def token_choice(lengths, choices):
    prompt_ends = jnp.cumsum(lengths)
    positions = jnp.arange(GROUP_TOK, dtype=jnp.int32)
    prompt_index = lax.optimization_barrier(jnp.sum((positions[:, None] >= prompt_ends[None, :]).astype(jnp.int32), axis=1))
    hits = prompt_index[:, None] == jnp.arange(PROMPTS, dtype=jnp.int32)[None, :]
    return lax.optimization_barrier(jnp.sum(jnp.where(hits, choices[None, :], 0), axis=1)).astype(jnp.int32)

def reference(resid, norm_gain, gate_weight_matrix, up_weight, w_down, gate_a, gate_b, up_a, up_b, down_a, down_b, prompt_lengths, prompt_choice, used_adapters, adapter_holder):
    slot_used = adapter_holder[used_adapters]
    gate_in = jnp.transpose(gate_a[slot_used], (1, 0, 2)).reshape(D, USED * RANK)
    up_in = jnp.transpose(up_a[slot_used], (1, 0, 2)).reshape(D, USED * RANK)
    down_in = jnp.transpose(down_a[slot_used], (1, 0, 2)).reshape(FF, USED * RANK)
    gate_output = gate_b[slot_used].reshape(USED * RANK, FF)
    up_output = up_b[slot_used].reshape(USED * RANK, FF)
    down_output = down_b[slot_used].reshape(USED * RANK, D)
    block_width = FF // N_TENSOR
    down_blocks = w_down.astype(jnp.float32).reshape(N_TENSOR, block_width, D)
    gain_f = norm_gain.astype(jnp.float32)

    def select(low_rank, weights):
        picked = lax.optimization_barrier(jnp.sum(low_rank.reshape(GROUP_TOK, USED, RANK) * weights[:, :, None], axis=1)).astype(jnp.bfloat16)
        spread = (picked[:, None, :].astype(jnp.float32) * weights[:, :, None]).astype(jnp.bfloat16)
        return spread.reshape(GROUP_TOK, USED * RANK)

    def one_group(inputs):
        resid_g, lengths, choices = inputs
        weights = (token_choice(lengths, choices)[:, None] == jnp.arange(USED, dtype=jnp.int32)[None, :]).astype(jnp.float32)
        residual_float = resid_g.astype(jnp.float32)
        scale = lax.rsqrt(lax.optimization_barrier(jnp.mean(residual_float * residual_float, axis=-1, keepdims=True)) + 1e-06)
        normalized_input = (residual_float * scale * gain_f).astype(jnp.bfloat16)
        gate_adapter_rows = select(jnp.dot(normalized_input, gate_in, preferred_element_type=jnp.float32), weights)
        up_adapter_rows = select(jnp.dot(normalized_input, up_in, preferred_element_type=jnp.float32), weights)
        gate_preactivation = jnp.dot(normalized_input, gate_weight_matrix, preferred_element_type=jnp.float32) + adapter_scale * jnp.dot(gate_adapter_rows, gate_output, preferred_element_type=jnp.float32)
        up_preactivation = jnp.dot(normalized_input, up_weight, preferred_element_type=jnp.float32) + adapter_scale * jnp.dot(up_adapter_rows, up_output, preferred_element_type=jnp.float32)
        hidden = (jax.nn.silu(gate_preactivation) * up_preactivation).astype(jnp.bfloat16)
        hidden_blocks = hidden.astype(jnp.float32).reshape(GROUP_TOK, N_TENSOR, block_width)
        partials = jnp.einsum('tkf,kfd->ktd', hidden_blocks, down_blocks, precision=lax.Precision.HIGHEST)
        partials = lax.optimization_barrier(partials.astype(jnp.bfloat16))
        down_total_sum = lax.optimization_barrier(jnp.sum(partials.astype(jnp.float32), axis=0))
        down_adapter_rows = select(jnp.dot(hidden, down_in, preferred_element_type=jnp.float32), weights)
        adapter_down_term = jnp.dot(down_adapter_rows, down_output, preferred_element_type=jnp.float32)
        return (residual_float + down_total_sum + adapter_scale * adapter_down_term).astype(jnp.bfloat16)
    return lax.map(one_group, (resid, prompt_lengths, prompt_choice))
```

```python
import jax
import jax.numpy as jnp
from jax import lax
from jax.sharding import PartitionSpec as P

adapter_scale = 0.5


def pick_rows(picker, stacked):
    flat = stacked.reshape(stacked.shape[0], -1)
    chosen = jnp.dot(picker, flat, preferred_element_type=jnp.float32).astype(jnp.bfloat16)
    return chosen.reshape((picker.shape[0],) + stacked.shape[1:])


def select_token(values, weights):
    return jnp.sum(values * weights[:, :, None], axis=1)


def local(
    resid,
    norm_gain,
    gate_weight_matrix,
    up_weight,
    w_down,
    gate_a,
    gate_b,
    up_a,
    up_b,
    down_a,
    down_b,
    prompt_lengths,
    prompt_choice,
    used_adapters,
    adapter_holder,
):
    tensor_n = lax.axis_size("tensor")
    tok_dev = resid.shape[1]
    d_model = resid.shape[2]
    group_tok = tok_dev * tensor_n
    used_n = used_adapters.shape[0]
    rank_n = gate_a.shape[2]
    feat_loc = gate_a.shape[1]
    slots_loc = gate_a.shape[0]
    hidden_local = gate_weight_matrix.shape[1]
    adapters_n = adapter_holder.shape[0]

    matches = used_adapters[:, None] == jnp.arange(adapters_n, dtype=jnp.int32)[None, :]
    slot_used = jnp.sum(jnp.where(matches, adapter_holder[None, :], 0), axis=1)
    picker = (slot_used[:, None] == jnp.arange(adapters_n, dtype=jnp.int32)[None, :]).astype(
        jnp.bfloat16
    )

    pieces = (gate_a, up_a, gate_b, up_b, down_a)
    widths = [p.shape[1] * p.shape[2] for p in pieces]
    pack = jnp.concatenate([p.reshape(slots_loc, -1) for p in pieces], axis=1)
    whole = lax.all_gather(pack, "seq", axis=0, tiled=True)
    chosen = pick_rows(picker, whole)
    offs = [0]
    for w in widths:
        offs.append(offs[-1] + w)
    sel = [
        chosen[:, offs[i] : offs[i + 1]].reshape((used_n,) + pieces[i].shape[1:])
        for i in range(len(pieces))
    ]
    sel_ga, sel_ua, sel_gb, sel_ub, sel_da = sel

    whole_db = lax.all_gather(down_b, "seq", axis=0, tiled=True)
    sel_db = pick_rows(picker, whole_db)

    prompt_ends = jnp.cumsum(prompt_lengths[0])
    positions = jnp.arange(group_tok, dtype=jnp.int32)
    prompt_index = jnp.sum((positions[:, None] >= prompt_ends[None, :]).astype(jnp.int32), axis=1)
    prompts_n = prompt_lengths.shape[1]
    hits = prompt_index[:, None] == jnp.arange(prompts_n, dtype=jnp.int32)[None, :]
    tok_choice = jnp.sum(jnp.where(hits, prompt_choice[0][None, :], 0), axis=1)
    token_weights = (tok_choice[:, None] == jnp.arange(used_n, dtype=jnp.int32)[None, :]).astype(
        jnp.float32
    )
    row_first = lax.axis_index("tensor") * tok_dev
    own_weights = lax.dynamic_slice_in_dim(token_weights, row_first, tok_dev, 0)

    residual_float = resid[0].astype(jnp.float32)
    scale = lax.rsqrt(jnp.mean(residual_float * residual_float, axis=-1, keepdims=True) + 1e-06)
    normalized_input = (residual_float * scale * norm_gain.astype(jnp.float32)).astype(jnp.bfloat16)

    tpack = jnp.concatenate(
        [normalized_input.reshape(-1), sel_ga.reshape(-1), sel_ua.reshape(-1)], axis=0
    )
    tall = lax.all_gather(tpack, "tensor", axis=0, tiled=False)
    n_tok_el = tok_dev * d_model
    n_a_el = used_n * feat_loc * rank_n
    piece = tall[:, :n_tok_el].reshape(group_tok, d_model)
    ga_all = tall[:, n_tok_el : n_tok_el + n_a_el].reshape(tensor_n, used_n, feat_loc, rank_n)
    ua_all = tall[:, n_tok_el + n_a_el :].reshape(tensor_n, used_n, feat_loc, rank_n)

    def to_cols(a):
        return jnp.transpose(a, (0, 2, 1, 3)).reshape(tensor_n * feat_loc, used_n * rank_n)

    both_in = jnp.concatenate([to_cols(ga_all), to_cols(ua_all)], axis=1)
    low = jnp.dot(piece, both_in, preferred_element_type=jnp.float32).reshape(
        group_tok, 2, used_n, rank_n
    )
    mid_gate = select_token(low[:, 0], token_weights).astype(jnp.bfloat16)
    mid_up = select_token(low[:, 1], token_weights).astype(jnp.bfloat16)
    weights_bf = token_weights.astype(jnp.bfloat16)

    def spread(mid):
        return (mid[:, None, :] * weights_bf[:, :, None]).reshape(group_tok, used_n * rank_n)

    gate_part = jnp.dot(piece, gate_weight_matrix, preferred_element_type=jnp.float32)
    up_part = jnp.dot(piece, up_weight, preferred_element_type=jnp.float32)
    gate_adapter_rows = jnp.dot(
        spread(mid_gate),
        sel_gb.reshape(used_n * rank_n, hidden_local),
        preferred_element_type=jnp.float32,
    )
    up_adapter_rows = jnp.dot(
        spread(mid_up),
        sel_ub.reshape(used_n * rank_n, hidden_local),
        preferred_element_type=jnp.float32,
    )
    gate_preactivation = gate_part + adapter_scale * gate_adapter_rows
    up_preactivation = up_part + adapter_scale * up_adapter_rows
    hidden = (jax.nn.silu(gate_preactivation) * up_preactivation).astype(jnp.bfloat16)

    down_part = jnp.dot(hidden, w_down, preferred_element_type=jnp.float32).astype(jnp.bfloat16)
    da_cols = jnp.transpose(sel_da, (1, 0, 2)).reshape(hidden_local, used_n * rank_n)
    down_adapter_rows = jnp.dot(hidden, da_cols, preferred_element_type=jnp.float32).reshape(
        group_tok, used_n, rank_n
    )
    partial_down = select_token(down_adapter_rows, token_weights).astype(jnp.bfloat16)

    joined = jnp.concatenate([down_part, partial_down], axis=1)
    reduced = lax.psum_scatter(joined, "tensor", scatter_dimension=0, tiled=True)
    down_total_sum = reduced[:, :d_model].astype(jnp.float32)
    mid_down = reduced[:, d_model:]

    spread_down = (mid_down[:, None, :] * own_weights.astype(jnp.bfloat16)[:, :, None]).reshape(
        tok_dev, used_n * rank_n
    )
    adapter_down_term = jnp.dot(
        spread_down,
        sel_db.reshape(used_n * rank_n, sel_db.shape[2]),
        preferred_element_type=jnp.float32,
    )
    return (residual_float + down_total_sum + adapter_scale * adapter_down_term).astype(
        jnp.bfloat16
    )[None]


def solution(mesh):
    placed = (
        P("seq", "tensor", None),
        P(),
        P(None, "tensor"),
        P(None, "tensor"),
        P("tensor", None),
        P("seq", "tensor", None),
        P("seq", None, "tensor"),
        P("seq", "tensor", None),
        P("seq", None, "tensor"),
        P("seq", "tensor", None),
        P("seq", None, None),
        P("seq", None),
        P("seq", None),
        P(),
        P(),
    )
    return jax.shard_map(
        local, mesh=mesh, in_specs=placed, out_specs=P("seq", "tensor", None), check_vma=False
    )
```

```python
import jax
import jax.numpy as jnp
from jax import lax
from jax.sharding import PartitionSpec as P

adapter_scale = 0.5


def pick_rows(picker, stacked):
    flat = stacked.reshape(stacked.shape[0], -1)
    chosen = jnp.dot(picker, flat, preferred_element_type=jnp.float32).astype(jnp.bfloat16)
    return chosen.reshape((picker.shape[0],) + stacked.shape[1:])


def select_token(values, weights):
    return jnp.sum(values * weights[:, :, None], axis=1)


def local(
    resid,
    norm_gain,
    gate_weight_matrix,
    up_weight,
    w_down,
    gate_a,
    gate_b,
    up_a,
    up_b,
    down_a,
    down_b,
    prompt_lengths,
    prompt_choice,
    used_adapters,
    adapter_holder,
):
    tensor_n = lax.axis_size("tensor")
    tok_dev = resid.shape[1]
    d_model = resid.shape[2]
    group_tok = tok_dev * tensor_n
    used_n = used_adapters.shape[0]
    rank_n = gate_a.shape[2]
    feat_loc = gate_a.shape[1]
    slots_loc = gate_a.shape[0]
    hidden_local = gate_weight_matrix.shape[1]
    adapters_n = adapter_holder.shape[0]

    matches = used_adapters[:, None] == jnp.arange(adapters_n, dtype=jnp.int32)[None, :]
    slot_used = jnp.sum(jnp.where(matches, adapter_holder[None, :], 0), axis=1)
    picker = (slot_used[:, None] == jnp.arange(adapters_n, dtype=jnp.int32)[None, :]).astype(
        jnp.bfloat16
    )

    col_n = d_model // tensor_n
    col_first = lax.axis_index("tensor") * col_n
    db_block = lax.dynamic_slice_in_dim(down_b, col_first, col_n, 2)
    pieces = (gate_a, up_a, gate_b, up_b, down_a, db_block)
    widths = [p.shape[1] * p.shape[2] for p in pieces]
    pack = jnp.concatenate([p.reshape(slots_loc, -1) for p in pieces], axis=1)
    whole = lax.all_gather(pack, "seq", axis=0, tiled=False)
    seq_n = whole.shape[0]
    picker3 = picker.reshape(used_n, seq_n, slots_loc)
    chosen = jnp.einsum(
        "ugs,gsx->ux", picker3, whole, preferred_element_type=jnp.float32
    ).astype(jnp.bfloat16)
    offs = [0]
    for w in widths:
        offs.append(offs[-1] + w)
    sel = [
        chosen[:, offs[i] : offs[i + 1]].reshape((used_n,) + pieces[i].shape[1:])
        for i in range(len(pieces))
    ]
    sel_ga, sel_ua, sel_gb, sel_ub, sel_da, sel_db = sel

    prompt_ends = jnp.cumsum(prompt_lengths[0])
    positions = jnp.arange(group_tok, dtype=jnp.int32)
    prompt_index = jnp.sum((positions[:, None] >= prompt_ends[None, :]).astype(jnp.int32), axis=1)
    prompts_n = prompt_lengths.shape[1]
    hits = prompt_index[:, None] == jnp.arange(prompts_n, dtype=jnp.int32)[None, :]
    tok_choice = jnp.sum(jnp.where(hits, prompt_choice[0][None, :], 0), axis=1)
    token_weights = (tok_choice[:, None] == jnp.arange(used_n, dtype=jnp.int32)[None, :]).astype(
        jnp.float32
    )
    row_first = lax.axis_index("tensor") * tok_dev
    own_weights = lax.dynamic_slice_in_dim(token_weights, row_first, tok_dev, 0)

    residual_float = resid[0].astype(jnp.float32)
    scale = lax.rsqrt(jnp.mean(residual_float * residual_float, axis=-1, keepdims=True) + 1e-06)
    normalized_input = (residual_float * scale * norm_gain.astype(jnp.float32)).astype(jnp.bfloat16)

    def feat_major(a):
        return jnp.transpose(a, (1, 0, 2)).reshape(feat_loc, used_n * rank_n)

    a_rows = jnp.concatenate([feat_major(sel_ga), feat_major(sel_ua)], axis=1).reshape(-1, d_model)
    db_rows = sel_db.reshape(-1, d_model)
    tpack = jnp.concatenate([normalized_input, a_rows, db_rows], axis=0)
    tall = lax.all_gather(tpack, "tensor", axis=0, tiled=False)
    r0 = tok_dev
    r1 = r0 + a_rows.shape[0]
    piece = tall[:, :r0].reshape(group_tok, d_model)
    both_in = tall[:, r0:r1].reshape(tensor_n * feat_loc, 2 * used_n * rank_n)
    db_all = tall[:, r1:].reshape(tensor_n, used_n * rank_n, col_n)

    low = jnp.dot(piece, both_in, preferred_element_type=jnp.float32).reshape(
        group_tok, 2, used_n, rank_n
    )
    mid_gate = select_token(low[:, 0], token_weights).astype(jnp.bfloat16)
    mid_up = select_token(low[:, 1], token_weights).astype(jnp.bfloat16)
    weights_bf = token_weights.astype(jnp.bfloat16)

    def spread(mid):
        return (mid[:, None, :] * weights_bf[:, :, None]).reshape(group_tok, used_n * rank_n)

    gate_part = jnp.dot(piece, gate_weight_matrix, preferred_element_type=jnp.float32)
    up_part = jnp.dot(piece, up_weight, preferred_element_type=jnp.float32)
    gate_adapter_rows = jnp.dot(
        spread(mid_gate),
        sel_gb.reshape(used_n * rank_n, hidden_local),
        preferred_element_type=jnp.float32,
    )
    up_adapter_rows = jnp.dot(
        spread(mid_up),
        sel_ub.reshape(used_n * rank_n, hidden_local),
        preferred_element_type=jnp.float32,
    )
    gate_preactivation = gate_part + adapter_scale * gate_adapter_rows
    up_preactivation = up_part + adapter_scale * up_adapter_rows
    hidden = (jax.nn.silu(gate_preactivation) * up_preactivation).astype(jnp.bfloat16)

    down_part = jnp.dot(hidden, w_down, preferred_element_type=jnp.float32).astype(jnp.bfloat16)
    da_cols = jnp.transpose(sel_da, (1, 0, 2)).reshape(hidden_local, used_n * rank_n)
    down_adapter_rows = jnp.dot(hidden, da_cols, preferred_element_type=jnp.float32).reshape(
        group_tok, used_n, rank_n
    )
    partial_down = select_token(down_adapter_rows, token_weights).astype(jnp.bfloat16)

    joined = jnp.concatenate([down_part, partial_down], axis=1)
    reduced = lax.psum_scatter(joined, "tensor", scatter_dimension=0, tiled=True)
    down_total_sum = reduced[:, :d_model].astype(jnp.float32)
    mid_down = reduced[:, d_model:]

    spread_down = (mid_down[:, None, :] * own_weights.astype(jnp.bfloat16)[:, :, None]).reshape(
        tok_dev, used_n * rank_n
    )
    adapter_down_term = jnp.einsum(
        "tk,jkc->tjc", spread_down, db_all, preferred_element_type=jnp.float32
    ).reshape(tok_dev, d_model)
    return (residual_float + down_total_sum + adapter_scale * adapter_down_term).astype(
        jnp.bfloat16
    )[None]


def solution(mesh):
    placed = (
        P("seq", "tensor", None),
        P(),
        P(None, "tensor"),
        P(None, "tensor"),
        P("tensor", None),
        P("seq", "tensor", None),
        P("seq", None, "tensor"),
        P("seq", "tensor", None),
        P("seq", None, "tensor"),
        P("seq", "tensor", None),
        P("seq", None, None),
        P("seq", None),
        P("seq", None),
        P(),
        P(),
    )
    return jax.shard_map(
        local, mesh=mesh, in_specs=placed, out_specs=P("seq", "tensor", None), check_vma=False
    )
```

```python
import jax
import jax.numpy as jnp
from jax import lax
from jax.sharding import PartitionSpec as P

adapter_scale = 0.5


def pick_rows(picker, stacked):
    flat = stacked.reshape(stacked.shape[0], -1)
    chosen = jnp.dot(picker, flat, preferred_element_type=jnp.float32).astype(jnp.bfloat16)
    return chosen.reshape((picker.shape[0],) + stacked.shape[1:])


def select_token(values, weights):
    return jnp.sum(values * weights[:, :, None], axis=1)


def reduce_scatter_rows(x, axis_name, axis_n):
    bits = axis_n.bit_length() - 1
    me = lax.axis_index(axis_name)
    rows = x.shape[0] // axis_n
    acc = x.astype(jnp.float32).reshape((2,) * bits + (rows,) + x.shape[1:])
    for b in range(bits):
        ax = bits - 1 - b
        mine = (me >> b) & 1
        keep = lax.dynamic_index_in_dim(acc, mine, axis=ax, keepdims=False)
        send = lax.dynamic_index_in_dim(acc, 1 - mine, axis=ax, keepdims=False)
        perm = [(i, i ^ (1 << b)) for i in range(axis_n)]
        got = lax.ppermute(send.astype(jnp.bfloat16), axis_name, perm)
        acc = keep + got.astype(jnp.float32)
    return acc


def local(
    resid,
    norm_gain,
    gate_weight_matrix,
    up_weight,
    w_down,
    gate_a,
    gate_b,
    up_a,
    up_b,
    down_a,
    down_b,
    prompt_lengths,
    prompt_choice,
    used_adapters,
    adapter_holder,
):
    tensor_n = lax.axis_size("tensor")
    tok_dev = resid.shape[1]
    d_model = resid.shape[2]
    group_tok = tok_dev * tensor_n
    used_n = used_adapters.shape[0]
    rank_n = gate_a.shape[2]
    feat_loc = gate_a.shape[1]
    slots_loc = gate_a.shape[0]
    hidden_local = gate_weight_matrix.shape[1]
    adapters_n = adapter_holder.shape[0]

    matches = used_adapters[:, None] == jnp.arange(adapters_n, dtype=jnp.int32)[None, :]
    slot_used = jnp.sum(jnp.where(matches, adapter_holder[None, :], 0), axis=1)
    picker = (slot_used[:, None] == jnp.arange(adapters_n, dtype=jnp.int32)[None, :]).astype(
        jnp.bfloat16
    )

    col_n = d_model // tensor_n
    col_first = lax.axis_index("tensor") * col_n
    db_block = lax.dynamic_slice_in_dim(down_b, col_first, col_n, 2)
    pieces = (gate_a, up_a, gate_b, up_b, down_a, db_block)
    widths = [p.shape[1] * p.shape[2] for p in pieces]
    pack = jnp.concatenate([p.reshape(slots_loc, -1) for p in pieces], axis=1)
    whole = lax.all_gather(pack, "seq", axis=0, tiled=False)
    seq_n = whole.shape[0]
    picker3 = picker.reshape(used_n, seq_n, slots_loc)
    chosen = jnp.einsum(
        "ugs,gsx->ux", picker3, whole, preferred_element_type=jnp.float32
    ).astype(jnp.bfloat16)
    offs = [0]
    for w in widths:
        offs.append(offs[-1] + w)
    sel = [
        chosen[:, offs[i] : offs[i + 1]].reshape((used_n,) + pieces[i].shape[1:])
        for i in range(len(pieces))
    ]
    sel_ga, sel_ua, sel_gb, sel_ub, sel_da, sel_db = sel

    prompt_ends = jnp.cumsum(prompt_lengths[0])
    positions = jnp.arange(group_tok, dtype=jnp.int32)
    prompt_index = jnp.sum((positions[:, None] >= prompt_ends[None, :]).astype(jnp.int32), axis=1)
    prompts_n = prompt_lengths.shape[1]
    hits = prompt_index[:, None] == jnp.arange(prompts_n, dtype=jnp.int32)[None, :]
    tok_choice = jnp.sum(jnp.where(hits, prompt_choice[0][None, :], 0), axis=1)
    token_weights = (tok_choice[:, None] == jnp.arange(used_n, dtype=jnp.int32)[None, :]).astype(
        jnp.float32
    )
    row_first = lax.axis_index("tensor") * tok_dev
    own_weights = lax.dynamic_slice_in_dim(token_weights, row_first, tok_dev, 0)

    residual_float = resid[0].astype(jnp.float32)
    scale = lax.rsqrt(jnp.mean(residual_float * residual_float, axis=-1, keepdims=True) + 1e-06)
    normalized_input = (residual_float * scale * norm_gain.astype(jnp.float32)).astype(jnp.bfloat16)

    def feat_major(a):
        return jnp.transpose(a, (1, 0, 2)).reshape(feat_loc, used_n * rank_n)

    a_rows = jnp.concatenate([feat_major(sel_ga), feat_major(sel_ua)], axis=1).reshape(-1, d_model)
    db_rows = sel_db.reshape(-1, d_model)
    tpack = jnp.concatenate([normalized_input, a_rows, db_rows], axis=0)
    tall = lax.all_gather(tpack, "tensor", axis=0, tiled=False)
    r0 = tok_dev
    r1 = r0 + a_rows.shape[0]
    piece = tall[:, :r0].reshape(group_tok, d_model)
    both_in = tall[:, r0:r1].reshape(tensor_n * feat_loc, 2 * used_n * rank_n)
    db_all = tall[:, r1:].reshape(tensor_n, used_n * rank_n, col_n)

    low = jnp.dot(piece, both_in, preferred_element_type=jnp.float32).reshape(
        group_tok, 2, used_n, rank_n
    )
    mid_gate = select_token(low[:, 0], token_weights).astype(jnp.bfloat16)
    mid_up = select_token(low[:, 1], token_weights).astype(jnp.bfloat16)
    weights_bf = token_weights.astype(jnp.bfloat16)

    def spread(mid):
        return (mid[:, None, :] * weights_bf[:, :, None]).reshape(group_tok, used_n * rank_n)

    gate_part = jnp.dot(piece, gate_weight_matrix, preferred_element_type=jnp.float32)
    up_part = jnp.dot(piece, up_weight, preferred_element_type=jnp.float32)
    gate_adapter_rows = jnp.dot(
        spread(mid_gate),
        sel_gb.reshape(used_n * rank_n, hidden_local),
        preferred_element_type=jnp.float32,
    )
    up_adapter_rows = jnp.dot(
        spread(mid_up),
        sel_ub.reshape(used_n * rank_n, hidden_local),
        preferred_element_type=jnp.float32,
    )
    gate_preactivation = gate_part + adapter_scale * gate_adapter_rows
    up_preactivation = up_part + adapter_scale * up_adapter_rows
    hidden = (jax.nn.silu(gate_preactivation) * up_preactivation).astype(jnp.bfloat16)

    down_part = jnp.dot(hidden, w_down, preferred_element_type=jnp.float32).astype(jnp.bfloat16)
    da_cols = jnp.transpose(sel_da, (1, 0, 2)).reshape(hidden_local, used_n * rank_n)
    down_adapter_rows = jnp.dot(hidden, da_cols, preferred_element_type=jnp.float32).reshape(
        group_tok, used_n, rank_n
    )
    partial_down = select_token(down_adapter_rows, token_weights).astype(jnp.bfloat16)

    joined = jnp.concatenate([down_part, partial_down], axis=1)
    reduced = reduce_scatter_rows(joined, "tensor", tensor_n)
    down_total_sum = reduced[:, :d_model]
    mid_down = reduced[:, d_model:].astype(jnp.bfloat16)

    spread_down = (mid_down[:, None, :] * own_weights.astype(jnp.bfloat16)[:, :, None]).reshape(
        tok_dev, used_n * rank_n
    )
    adapter_down_term = jnp.einsum(
        "tk,jkc->tjc", spread_down, db_all, preferred_element_type=jnp.float32
    ).reshape(tok_dev, d_model)
    return (residual_float + down_total_sum + adapter_scale * adapter_down_term).astype(
        jnp.bfloat16
    )[None]


def solution(mesh):
    placed = (
        P("seq", "tensor", None),
        P(),
        P(None, "tensor"),
        P(None, "tensor"),
        P("tensor", None),
        P("seq", "tensor", None),
        P("seq", None, "tensor"),
        P("seq", "tensor", None),
        P("seq", None, "tensor"),
        P("seq", "tensor", None),
        P("seq", None, None),
        P("seq", None),
        P("seq", None),
        P(),
        P(),
    )
    return jax.shard_map(
        local, mesh=mesh, in_specs=placed, out_specs=P("seq", "tensor", None), check_vma=False
    )
```

```python
import jax
import jax.numpy as jnp
from jax import lax
from jax.sharding import PartitionSpec as P

adapter_scale = 0.5


def pick_rows(picker, stacked):
    flat = stacked.reshape(stacked.shape[0], -1)
    chosen = jnp.dot(picker, flat, preferred_element_type=jnp.float32).astype(jnp.bfloat16)
    return chosen.reshape((picker.shape[0],) + stacked.shape[1:])


def select_token(values, weights):
    return jnp.sum(values * weights[:, :, None], axis=1)


def reduce_scatter_rows(x, axis_name, axis_n):
    bits = axis_n.bit_length() - 1
    me = lax.axis_index(axis_name)
    rows = x.shape[0] // axis_n
    acc = x.astype(jnp.float32).reshape((2,) * bits + (rows,) + x.shape[1:])
    for b in range(bits):
        ax = bits - 1 - b
        mine = (me >> b) & 1
        keep = lax.dynamic_index_in_dim(acc, mine, axis=ax, keepdims=False)
        send = lax.dynamic_index_in_dim(acc, 1 - mine, axis=ax, keepdims=False)
        perm = [(i, i ^ (1 << b)) for i in range(axis_n)]
        got = lax.ppermute(send.astype(jnp.bfloat16), axis_name, perm)
        acc = keep + got.astype(jnp.float32)
    return acc


def all_gather_rows(x, axis_name, axis_n):
    bits = axis_n.bit_length() - 1
    me = lax.axis_index(axis_name)
    acc = x
    for k, b in enumerate(reversed(range(bits))):
        mine = (me >> b) & 1
        perm = [(i, i ^ (1 << b)) for i in range(axis_n)]
        got = lax.ppermute(acc, axis_name, perm)
        lo = jnp.where(mine == 0, acc, got)
        hi = jnp.where(mine == 0, got, acc)
        acc = jnp.stack([lo, hi], axis=k)
    return acc.reshape((axis_n * x.shape[0],) + x.shape[1:])


def all_reduce_sum(x, axis_name, axis_n):
    bits = axis_n.bit_length() - 1
    acc = x
    for b in range(bits):
        perm = [(i, i ^ (1 << b)) for i in range(axis_n)]
        acc = acc + lax.ppermute(acc, axis_name, perm)
    return acc


def local(
    resid,
    norm_gain,
    gate_weight_matrix,
    up_weight,
    w_down,
    gate_a,
    gate_b,
    up_a,
    up_b,
    down_a,
    down_b,
    prompt_lengths,
    prompt_choice,
    used_adapters,
    adapter_holder,
):
    tensor_n = lax.axis_size("tensor")
    tok_dev = resid.shape[1]
    d_model = resid.shape[2]
    group_tok = tok_dev * tensor_n
    used_n = used_adapters.shape[0]
    rank_n = gate_a.shape[2]
    feat_loc = gate_a.shape[1]
    slots_loc = gate_a.shape[0]
    hidden_local = gate_weight_matrix.shape[1]
    adapters_n = adapter_holder.shape[0]

    matches = used_adapters[:, None] == jnp.arange(adapters_n, dtype=jnp.int32)[None, :]
    slot_used = jnp.sum(jnp.where(matches, adapter_holder[None, :], 0), axis=1)
    picker = (slot_used[:, None] == jnp.arange(adapters_n, dtype=jnp.int32)[None, :]).astype(
        jnp.bfloat16
    )

    col_n = d_model // tensor_n
    col_first = lax.axis_index("tensor") * col_n
    db_block = lax.dynamic_slice_in_dim(down_b, col_first, col_n, 2)
    pieces = (gate_a, up_a, gate_b, up_b, down_a, db_block)
    widths = [p.shape[1] * p.shape[2] for p in pieces]
    pack = jnp.concatenate([p.reshape(slots_loc, -1) for p in pieces], axis=1)
    whole = lax.all_gather(pack, "seq", axis=0, tiled=False)
    seq_n = whole.shape[0]
    picker3 = picker.reshape(used_n, seq_n, slots_loc)
    chosen = jnp.einsum(
        "ugs,gsx->ux", picker3, whole, preferred_element_type=jnp.float32
    ).astype(jnp.bfloat16)
    offs = [0]
    for w in widths:
        offs.append(offs[-1] + w)
    sel = [
        chosen[:, offs[i] : offs[i + 1]].reshape((used_n,) + pieces[i].shape[1:])
        for i in range(len(pieces))
    ]
    sel_ga, sel_ua, sel_gb, sel_ub, sel_da, sel_db = sel

    prompt_ends = jnp.cumsum(prompt_lengths[0])
    positions = jnp.arange(group_tok, dtype=jnp.int32)
    prompt_index = jnp.sum((positions[:, None] >= prompt_ends[None, :]).astype(jnp.int32), axis=1)
    prompts_n = prompt_lengths.shape[1]
    hits = prompt_index[:, None] == jnp.arange(prompts_n, dtype=jnp.int32)[None, :]
    tok_choice = jnp.sum(jnp.where(hits, prompt_choice[0][None, :], 0), axis=1)
    token_weights = (tok_choice[:, None] == jnp.arange(used_n, dtype=jnp.int32)[None, :]).astype(
        jnp.float32
    )
    row_first = lax.axis_index("tensor") * tok_dev
    own_weights = lax.dynamic_slice_in_dim(token_weights, row_first, tok_dev, 0)

    residual_float = resid[0].astype(jnp.float32)
    scale = lax.rsqrt(jnp.mean(residual_float * residual_float, axis=-1, keepdims=True) + 1e-06)
    normalized_input = (residual_float * scale * norm_gain.astype(jnp.float32)).astype(jnp.bfloat16)

    piece = all_gather_rows(normalized_input, "tensor", tensor_n)

    db_rows = sel_db.reshape(-1, d_model)
    db_all = lax.all_gather(db_rows, "tensor", axis=0, tiled=False).reshape(
        tensor_n, used_n * rank_n, col_n
    )

    def feat_major(a):
        return jnp.transpose(a, (1, 0, 2)).reshape(feat_loc, used_n * rank_n)

    both_in = jnp.concatenate([feat_major(sel_ga), feat_major(sel_ua)], axis=1)
    feat_first = lax.axis_index("tensor") * feat_loc
    own_cols = lax.dynamic_slice_in_dim(piece, feat_first, feat_loc, 1)
    low = jnp.dot(own_cols, both_in, preferred_element_type=jnp.float32).reshape(
        group_tok, 2, used_n, rank_n
    )
    partial_mid = jnp.sum(low * token_weights[:, None, :, None], axis=2)
    mids = all_reduce_sum(partial_mid, "tensor", tensor_n)
    mid_gate = mids[:, 0].astype(jnp.bfloat16)
    mid_up = mids[:, 1].astype(jnp.bfloat16)
    weights_bf = token_weights.astype(jnp.bfloat16)

    def spread(mid):
        return (mid[:, None, :] * weights_bf[:, :, None]).reshape(group_tok, used_n * rank_n)

    gate_part = jnp.dot(piece, gate_weight_matrix, preferred_element_type=jnp.float32)
    up_part = jnp.dot(piece, up_weight, preferred_element_type=jnp.float32)
    gate_adapter_rows = jnp.dot(
        spread(mid_gate),
        sel_gb.reshape(used_n * rank_n, hidden_local),
        preferred_element_type=jnp.float32,
    )
    up_adapter_rows = jnp.dot(
        spread(mid_up),
        sel_ub.reshape(used_n * rank_n, hidden_local),
        preferred_element_type=jnp.float32,
    )
    gate_preactivation = gate_part + adapter_scale * gate_adapter_rows
    up_preactivation = up_part + adapter_scale * up_adapter_rows
    hidden = (jax.nn.silu(gate_preactivation) * up_preactivation).astype(jnp.bfloat16)

    down_part = jnp.dot(hidden, w_down, preferred_element_type=jnp.float32).astype(jnp.bfloat16)
    da_cols = jnp.transpose(sel_da, (1, 0, 2)).reshape(hidden_local, used_n * rank_n)
    down_adapter_rows = jnp.dot(hidden, da_cols, preferred_element_type=jnp.float32).reshape(
        group_tok, used_n, rank_n
    )
    partial_down = select_token(down_adapter_rows, token_weights).astype(jnp.bfloat16)

    joined = jnp.concatenate([down_part, partial_down], axis=1)
    reduced = reduce_scatter_rows(joined, "tensor", tensor_n)
    down_total_sum = reduced[:, :d_model]
    mid_down = reduced[:, d_model:].astype(jnp.bfloat16)

    spread_down = (mid_down[:, None, :] * own_weights.astype(jnp.bfloat16)[:, :, None]).reshape(
        tok_dev, used_n * rank_n
    )
    adapter_down_term = jnp.einsum(
        "tk,jkc->tjc", spread_down, db_all, preferred_element_type=jnp.float32
    ).reshape(tok_dev, d_model)
    return (residual_float + down_total_sum + adapter_scale * adapter_down_term).astype(
        jnp.bfloat16
    )[None]


def solution(mesh):
    placed = (
        P("seq", "tensor", None),
        P(),
        P(None, "tensor"),
        P(None, "tensor"),
        P("tensor", None),
        P("seq", "tensor", None),
        P("seq", None, "tensor"),
        P("seq", "tensor", None),
        P("seq", None, "tensor"),
        P("seq", "tensor", None),
        P("seq", None, None),
        P("seq", None),
        P("seq", None),
        P(),
        P(),
    )
    return jax.shard_map(
        local, mesh=mesh, in_specs=placed, out_specs=P("seq", "tensor", None), check_vma=False
    )
```

```python
import jax
import jax.numpy as jnp
from jax import lax
from jax.sharding import PartitionSpec as P

adapter_scale = 0.5


def pick_rows(picker, stacked):
    flat = stacked.reshape(stacked.shape[0], -1)
    chosen = jnp.dot(picker, flat, preferred_element_type=jnp.float32).astype(jnp.bfloat16)
    return chosen.reshape((picker.shape[0],) + stacked.shape[1:])


def select_token(values, weights):
    return jnp.sum(values * weights[:, :, None], axis=1)


def reduce_scatter_rows(x, axis_name, axis_n):
    bits = axis_n.bit_length() - 1
    me = lax.axis_index(axis_name)
    rows = x.shape[0] // axis_n
    acc = x.astype(jnp.float32).reshape((2,) * bits + (rows,) + x.shape[1:])
    for b in range(bits):
        ax = bits - 1 - b
        mine = (me >> b) & 1
        keep = lax.dynamic_index_in_dim(acc, mine, axis=ax, keepdims=False)
        send = lax.dynamic_index_in_dim(acc, 1 - mine, axis=ax, keepdims=False)
        perm = [(i, i ^ (1 << b)) for i in range(axis_n)]
        got = lax.ppermute(send.astype(jnp.bfloat16), axis_name, perm)
        acc = keep + got.astype(jnp.float32)
    return acc


def all_gather_rows(x, axis_name, axis_n):
    bits = axis_n.bit_length() - 1
    me = lax.axis_index(axis_name)
    acc = x
    for k, b in enumerate(reversed(range(bits))):
        mine = (me >> b) & 1
        perm = [(i, i ^ (1 << b)) for i in range(axis_n)]
        got = lax.ppermute(acc, axis_name, perm)
        lo = jnp.where(mine == 0, acc, got)
        hi = jnp.where(mine == 0, got, acc)
        acc = jnp.stack([lo, hi], axis=k)
    return acc.reshape((axis_n * x.shape[0],) + x.shape[1:])


def all_reduce_sum(x, axis_name, axis_n):
    bits = axis_n.bit_length() - 1
    acc = x
    for b in range(bits):
        perm = [(i, i ^ (1 << b)) for i in range(axis_n)]
        acc = acc + lax.ppermute(acc, axis_name, perm)
    return acc


def local(
    resid,
    norm_gain,
    gate_weight_matrix,
    up_weight,
    w_down,
    gate_a,
    gate_b,
    up_a,
    up_b,
    down_a,
    down_b,
    prompt_lengths,
    prompt_choice,
    used_adapters,
    adapter_holder,
):
    tensor_n = lax.axis_size("tensor")
    tok_dev = resid.shape[1]
    d_model = resid.shape[2]
    group_tok = tok_dev * tensor_n
    used_n = used_adapters.shape[0]
    rank_n = gate_a.shape[2]
    feat_loc = gate_a.shape[1]
    slots_loc = gate_a.shape[0]
    hidden_local = gate_weight_matrix.shape[1]
    adapters_n = adapter_holder.shape[0]

    matches = used_adapters[:, None] == jnp.arange(adapters_n, dtype=jnp.int32)[None, :]
    slot_used = jnp.sum(jnp.where(matches, adapter_holder[None, :], 0), axis=1)
    picker = (slot_used[:, None] == jnp.arange(adapters_n, dtype=jnp.int32)[None, :]).astype(
        jnp.bfloat16
    )

    col_n = d_model // tensor_n
    col_first = lax.axis_index("tensor") * col_n
    db_block = lax.dynamic_slice_in_dim(down_b, col_first, col_n, 2)
    pieces = (gate_a, up_a, gate_b, up_b, down_a, db_block)
    widths = [p.shape[1] * p.shape[2] for p in pieces]
    pack = jnp.concatenate([p.reshape(slots_loc, -1) for p in pieces], axis=1)
    seq_n = lax.axis_size("seq")
    whole = all_gather_rows(pack, "seq", seq_n).reshape((seq_n,) + pack.shape)
    picker3 = picker.reshape(used_n, seq_n, slots_loc)
    chosen = jnp.einsum(
        "ugs,gsx->ux", picker3, whole, preferred_element_type=jnp.float32
    ).astype(jnp.bfloat16)
    offs = [0]
    for w in widths:
        offs.append(offs[-1] + w)
    sel = [
        chosen[:, offs[i] : offs[i + 1]].reshape((used_n,) + pieces[i].shape[1:])
        for i in range(len(pieces))
    ]
    sel_ga, sel_ua, sel_gb, sel_ub, sel_da, sel_db = sel

    prompt_ends = jnp.cumsum(prompt_lengths[0])
    positions = jnp.arange(group_tok, dtype=jnp.int32)
    prompt_index = jnp.sum((positions[:, None] >= prompt_ends[None, :]).astype(jnp.int32), axis=1)
    prompts_n = prompt_lengths.shape[1]
    hits = prompt_index[:, None] == jnp.arange(prompts_n, dtype=jnp.int32)[None, :]
    tok_choice = jnp.sum(jnp.where(hits, prompt_choice[0][None, :], 0), axis=1)
    token_weights = (tok_choice[:, None] == jnp.arange(used_n, dtype=jnp.int32)[None, :]).astype(
        jnp.float32
    )
    row_first = lax.axis_index("tensor") * tok_dev
    own_weights = lax.dynamic_slice_in_dim(token_weights, row_first, tok_dev, 0)

    residual_float = resid[0].astype(jnp.float32)
    scale = lax.rsqrt(jnp.mean(residual_float * residual_float, axis=-1, keepdims=True) + 1e-06)
    normalized_input = (residual_float * scale * norm_gain.astype(jnp.float32)).astype(jnp.bfloat16)

    piece = all_gather_rows(normalized_input, "tensor", tensor_n)

    db_rows = sel_db.reshape(-1, d_model)
    db_all = lax.all_gather(db_rows, "tensor", axis=0, tiled=False).reshape(
        tensor_n, used_n * rank_n, col_n
    )

    def feat_major(a):
        return jnp.transpose(a, (1, 0, 2)).reshape(feat_loc, used_n * rank_n)

    both_in = jnp.concatenate([feat_major(sel_ga), feat_major(sel_ua)], axis=1)
    feat_first = lax.axis_index("tensor") * feat_loc
    own_cols = lax.dynamic_slice_in_dim(piece, feat_first, feat_loc, 1)
    low = jnp.dot(own_cols, both_in, preferred_element_type=jnp.float32).reshape(
        group_tok, 2, used_n, rank_n
    )
    partial_mid = jnp.sum(low * token_weights[:, None, :, None], axis=2)
    mids = all_reduce_sum(partial_mid, "tensor", tensor_n)
    mid_gate = mids[:, 0].astype(jnp.bfloat16)
    mid_up = mids[:, 1].astype(jnp.bfloat16)
    weights_bf = token_weights.astype(jnp.bfloat16)

    def spread(mid):
        return (mid[:, None, :] * weights_bf[:, :, None]).reshape(group_tok, used_n * rank_n)

    gate_part = jnp.dot(piece, gate_weight_matrix, preferred_element_type=jnp.float32)
    up_part = jnp.dot(piece, up_weight, preferred_element_type=jnp.float32)
    gate_adapter_rows = jnp.dot(
        spread(mid_gate),
        sel_gb.reshape(used_n * rank_n, hidden_local),
        preferred_element_type=jnp.float32,
    )
    up_adapter_rows = jnp.dot(
        spread(mid_up),
        sel_ub.reshape(used_n * rank_n, hidden_local),
        preferred_element_type=jnp.float32,
    )
    gate_preactivation = gate_part + adapter_scale * gate_adapter_rows
    up_preactivation = up_part + adapter_scale * up_adapter_rows
    hidden = (jax.nn.silu(gate_preactivation) * up_preactivation).astype(jnp.bfloat16)

    down_part = jnp.dot(hidden, w_down, preferred_element_type=jnp.float32).astype(jnp.bfloat16)
    da_cols = jnp.transpose(sel_da, (1, 0, 2)).reshape(hidden_local, used_n * rank_n)
    down_adapter_rows = jnp.dot(hidden, da_cols, preferred_element_type=jnp.float32).reshape(
        group_tok, used_n, rank_n
    )
    partial_down = select_token(down_adapter_rows, token_weights).astype(jnp.bfloat16)

    joined = jnp.concatenate([down_part, partial_down], axis=1)
    reduced = reduce_scatter_rows(joined, "tensor", tensor_n)
    down_total_sum = reduced[:, :d_model]
    mid_down = reduced[:, d_model:].astype(jnp.bfloat16)

    spread_down = (mid_down[:, None, :] * own_weights.astype(jnp.bfloat16)[:, :, None]).reshape(
        tok_dev, used_n * rank_n
    )
    adapter_down_term = jnp.einsum(
        "tk,jkc->tjc", spread_down, db_all, preferred_element_type=jnp.float32
    ).reshape(tok_dev, d_model)
    return (residual_float + down_total_sum + adapter_scale * adapter_down_term).astype(
        jnp.bfloat16
    )[None]


def solution(mesh):
    placed = (
        P("seq", "tensor", None),
        P(),
        P(None, "tensor"),
        P(None, "tensor"),
        P("tensor", None),
        P("seq", "tensor", None),
        P("seq", None, "tensor"),
        P("seq", "tensor", None),
        P("seq", None, "tensor"),
        P("seq", "tensor", None),
        P("seq", None, None),
        P("seq", None),
        P("seq", None),
        P(),
        P(),
    )
    return jax.shard_map(
        local, mesh=mesh, in_specs=placed, out_specs=P("seq", "tensor", None), check_vma=False
    )
```

```python
import jax
import jax.numpy as jnp
from jax import lax
from jax.sharding import PartitionSpec as P

adapter_scale = 0.5


def pick_rows(picker, stacked):
    flat = stacked.reshape(stacked.shape[0], -1)
    chosen = jnp.dot(picker, flat, preferred_element_type=jnp.float32).astype(jnp.bfloat16)
    return chosen.reshape((picker.shape[0],) + stacked.shape[1:])


def select_token(values, weights):
    return jnp.sum(values * weights[:, :, None], axis=1)


def exchange_levels(bits):
    if bits % 2 == 1:
        return [(0, 1)] + [(s, 2) for s in range(1, bits, 2)]
    return [(s, 1) for s in range(bits)]


def group_perm(axis_n, shift, size, d):
    return [
        (i, i + ((((i >> shift) + d) % size - (i >> shift) % size) << shift)) for i in range(axis_n)
    ]


def reduce_scatter_rows(x, axis_name, axis_n):
    bits = axis_n.bit_length() - 1
    me = lax.axis_index(axis_name)
    rows = x.shape[0] // axis_n
    acc = x.astype(jnp.float32).reshape((2,) * bits + (rows,) + x.shape[1:])
    left = bits
    for shift, nb in exchange_levels(bits):
        size = 1 << nb
        ax = left - nb
        acc = acc.reshape((2,) * ax + (size,) + acc.shape[left:])
        mine = (me >> shift) % size
        total = lax.dynamic_index_in_dim(acc, mine, axis=ax, keepdims=False)
        for d in range(1, size):
            send = lax.dynamic_index_in_dim(acc, (mine + d) % size, axis=ax, keepdims=False)
            got = lax.ppermute(
                send.astype(jnp.bfloat16), axis_name, group_perm(axis_n, shift, size, d)
            )
            total = total + got.astype(jnp.float32)
        acc = total
        left = ax
    return acc


def all_gather_rows(x, axis_name, axis_n):
    bits = axis_n.bit_length() - 1
    me = lax.axis_index(axis_name)
    acc = x
    for k, b in enumerate(reversed(range(bits))):
        mine = (me >> b) & 1
        perm = [(i, i ^ (1 << b)) for i in range(axis_n)]
        got = lax.ppermute(acc, axis_name, perm)
        lo = jnp.where(mine == 0, acc, got)
        hi = jnp.where(mine == 0, got, acc)
        acc = jnp.stack([lo, hi], axis=k)
    return acc.reshape((axis_n * x.shape[0],) + x.shape[1:])


def all_reduce_sum(x, axis_name, axis_n):
    bits = axis_n.bit_length() - 1
    acc = x
    for shift, nb in exchange_levels(bits):
        size = 1 << nb
        total = acc
        for d in range(1, size):
            total = total + lax.ppermute(acc, axis_name, group_perm(axis_n, shift, size, d))
        acc = total
    return acc


def local(
    resid,
    norm_gain,
    gate_weight_matrix,
    up_weight,
    w_down,
    gate_a,
    gate_b,
    up_a,
    up_b,
    down_a,
    down_b,
    prompt_lengths,
    prompt_choice,
    used_adapters,
    adapter_holder,
):
    tensor_n = lax.axis_size("tensor")
    tok_dev = resid.shape[1]
    d_model = resid.shape[2]
    group_tok = tok_dev * tensor_n
    used_n = used_adapters.shape[0]
    rank_n = gate_a.shape[2]
    feat_loc = gate_a.shape[1]
    slots_loc = gate_a.shape[0]
    hidden_local = gate_weight_matrix.shape[1]
    adapters_n = adapter_holder.shape[0]

    matches = used_adapters[:, None] == jnp.arange(adapters_n, dtype=jnp.int32)[None, :]
    slot_used = jnp.sum(jnp.where(matches, adapter_holder[None, :], 0), axis=1)
    picker = (slot_used[:, None] == jnp.arange(adapters_n, dtype=jnp.int32)[None, :]).astype(
        jnp.bfloat16
    )

    col_n = d_model // tensor_n
    col_first = lax.axis_index("tensor") * col_n
    db_block = lax.dynamic_slice_in_dim(down_b, col_first, col_n, 2)
    pieces = (gate_a, up_a, gate_b, up_b, down_a, db_block)
    widths = [p.shape[1] * p.shape[2] for p in pieces]
    pack = jnp.concatenate([p.reshape(slots_loc, -1) for p in pieces], axis=1)
    whole = lax.all_gather(pack, "seq", axis=0, tiled=False)
    seq_n = whole.shape[0]
    picker3 = picker.reshape(used_n, seq_n, slots_loc)
    chosen = jnp.einsum(
        "ugs,gsx->ux", picker3, whole, preferred_element_type=jnp.float32
    ).astype(jnp.bfloat16)
    offs = [0]
    for w in widths:
        offs.append(offs[-1] + w)
    sel = [
        chosen[:, offs[i] : offs[i + 1]].reshape((used_n,) + pieces[i].shape[1:])
        for i in range(len(pieces))
    ]
    sel_ga, sel_ua, sel_gb, sel_ub, sel_da, sel_db = sel

    prompt_ends = jnp.cumsum(prompt_lengths[0])
    positions = jnp.arange(group_tok, dtype=jnp.int32)
    prompt_index = jnp.sum((positions[:, None] >= prompt_ends[None, :]).astype(jnp.int32), axis=1)
    prompts_n = prompt_lengths.shape[1]
    hits = prompt_index[:, None] == jnp.arange(prompts_n, dtype=jnp.int32)[None, :]
    tok_choice = jnp.sum(jnp.where(hits, prompt_choice[0][None, :], 0), axis=1)
    token_weights = (tok_choice[:, None] == jnp.arange(used_n, dtype=jnp.int32)[None, :]).astype(
        jnp.float32
    )
    row_first = lax.axis_index("tensor") * tok_dev
    own_weights = lax.dynamic_slice_in_dim(token_weights, row_first, tok_dev, 0)

    residual_float = resid[0].astype(jnp.float32)
    scale = lax.rsqrt(jnp.mean(residual_float * residual_float, axis=-1, keepdims=True) + 1e-06)
    normalized_input = (residual_float * scale * norm_gain.astype(jnp.float32)).astype(jnp.bfloat16)

    piece = all_gather_rows(normalized_input, "tensor", tensor_n)

    db_rows = sel_db.reshape(-1, d_model)
    db_all = lax.all_gather(db_rows, "tensor", axis=0, tiled=False).reshape(
        tensor_n, used_n * rank_n, col_n
    )

    def feat_major(a):
        return jnp.transpose(a, (1, 0, 2)).reshape(feat_loc, used_n * rank_n)

    both_in = jnp.concatenate([feat_major(sel_ga), feat_major(sel_ua)], axis=1)
    feat_first = lax.axis_index("tensor") * feat_loc
    own_cols = lax.dynamic_slice_in_dim(piece, feat_first, feat_loc, 1)
    low = jnp.dot(own_cols, both_in, preferred_element_type=jnp.float32).reshape(
        group_tok, 2, used_n, rank_n
    )
    partial_mid = jnp.sum(low * token_weights[:, None, :, None], axis=2)
    mids = all_reduce_sum(partial_mid, "tensor", tensor_n)
    mid_gate = mids[:, 0].astype(jnp.bfloat16)
    mid_up = mids[:, 1].astype(jnp.bfloat16)
    weights_bf = token_weights.astype(jnp.bfloat16)

    def spread(mid):
        return (mid[:, None, :] * weights_bf[:, :, None]).reshape(group_tok, used_n * rank_n)

    gate_part = jnp.dot(piece, gate_weight_matrix, preferred_element_type=jnp.float32)
    up_part = jnp.dot(piece, up_weight, preferred_element_type=jnp.float32)
    gate_adapter_rows = jnp.dot(
        spread(mid_gate),
        sel_gb.reshape(used_n * rank_n, hidden_local),
        preferred_element_type=jnp.float32,
    )
    up_adapter_rows = jnp.dot(
        spread(mid_up),
        sel_ub.reshape(used_n * rank_n, hidden_local),
        preferred_element_type=jnp.float32,
    )
    gate_preactivation = gate_part + adapter_scale * gate_adapter_rows
    up_preactivation = up_part + adapter_scale * up_adapter_rows
    hidden = (jax.nn.silu(gate_preactivation) * up_preactivation).astype(jnp.bfloat16)

    down_part = jnp.dot(hidden, w_down, preferred_element_type=jnp.float32).astype(jnp.bfloat16)
    da_cols = jnp.transpose(sel_da, (1, 0, 2)).reshape(hidden_local, used_n * rank_n)
    down_adapter_rows = jnp.dot(hidden, da_cols, preferred_element_type=jnp.float32).reshape(
        group_tok, used_n, rank_n
    )
    partial_down = select_token(down_adapter_rows, token_weights).astype(jnp.bfloat16)

    joined = jnp.concatenate([down_part, partial_down], axis=1)
    reduced = reduce_scatter_rows(joined, "tensor", tensor_n)
    down_total_sum = reduced[:, :d_model]
    mid_down = reduced[:, d_model:].astype(jnp.bfloat16)

    spread_down = (mid_down[:, None, :] * own_weights.astype(jnp.bfloat16)[:, :, None]).reshape(
        tok_dev, used_n * rank_n
    )
    adapter_down_term = jnp.einsum(
        "tk,jkc->tjc", spread_down, db_all, preferred_element_type=jnp.float32
    ).reshape(tok_dev, d_model)
    return (residual_float + down_total_sum + adapter_scale * adapter_down_term).astype(
        jnp.bfloat16
    )[None]


def solution(mesh):
    placed = (
        P("seq", "tensor", None),
        P(),
        P(None, "tensor"),
        P(None, "tensor"),
        P("tensor", None),
        P("seq", "tensor", None),
        P("seq", None, "tensor"),
        P("seq", "tensor", None),
        P("seq", None, "tensor"),
        P("seq", "tensor", None),
        P("seq", None, None),
        P("seq", None),
        P("seq", None),
        P(),
        P(),
    )
    return jax.shard_map(
        local, mesh=mesh, in_specs=placed, out_specs=P("seq", "tensor", None), check_vma=False
    )
```

```python
import jax
import jax.numpy as jnp
from jax import lax
from jax.sharding import PartitionSpec as P

adapter_scale = 0.5


def pick_rows(picker, stacked):
    flat = stacked.reshape(stacked.shape[0], -1)
    chosen = jnp.dot(picker, flat, preferred_element_type=jnp.float32).astype(jnp.bfloat16)
    return chosen.reshape((picker.shape[0],) + stacked.shape[1:])


def select_token(values, weights):
    return jnp.sum(values * weights[:, :, None], axis=1)


def exchange_levels(bits):
    if bits % 2 == 1:
        return [(0, 1)] + [(s, 2) for s in range(1, bits, 2)]
    return [(s, 1) for s in range(bits)]


def group_perm(axis_n, shift, size, d):
    return [
        (i, i + ((((i >> shift) + d) % size - (i >> shift) % size) << shift)) for i in range(axis_n)
    ]


def reduce_scatter_rows(x, axis_name, axis_n):
    bits = axis_n.bit_length() - 1
    me = lax.axis_index(axis_name)
    rows = x.shape[0] // axis_n
    acc = x.astype(jnp.float32).reshape((2,) * bits + (rows,) + x.shape[1:])
    left = bits
    for shift, nb in exchange_levels(bits):
        size = 1 << nb
        ax = left - nb
        acc = acc.reshape((2,) * ax + (size,) + acc.shape[left:])
        mine = (me >> shift) % size
        total = lax.dynamic_index_in_dim(acc, mine, axis=ax, keepdims=False)
        for d in range(1, size):
            send = lax.dynamic_index_in_dim(acc, (mine + d) % size, axis=ax, keepdims=False)
            got = lax.ppermute(
                send.astype(jnp.bfloat16), axis_name, group_perm(axis_n, shift, size, d)
            )
            total = total + got.astype(jnp.float32)
        acc = total
        left = ax
    return acc


def all_gather_rows(x, axis_name, axis_n):
    bits = axis_n.bit_length() - 1
    me = lax.axis_index(axis_name)
    acc = x
    for k, b in enumerate(reversed(range(bits))):
        mine = (me >> b) & 1
        perm = [(i, i ^ (1 << b)) for i in range(axis_n)]
        got = lax.ppermute(acc, axis_name, perm)
        lo = jnp.where(mine == 0, acc, got)
        hi = jnp.where(mine == 0, got, acc)
        acc = jnp.stack([lo, hi], axis=k)
    return acc.reshape((axis_n * x.shape[0],) + x.shape[1:])


def all_reduce_sum(x, axis_name, axis_n):
    bits = axis_n.bit_length() - 1
    acc = x
    for shift, nb in exchange_levels(bits):
        size = 1 << nb
        total = acc
        for d in range(1, size):
            total = total + lax.ppermute(acc, axis_name, group_perm(axis_n, shift, size, d))
        acc = total
    return acc


def local(
    resid,
    norm_gain,
    gate_weight_matrix,
    up_weight,
    w_down,
    gate_a,
    gate_b,
    up_a,
    up_b,
    down_a,
    down_b,
    prompt_lengths,
    prompt_choice,
    used_adapters,
    adapter_holder,
):
    tensor_n = lax.axis_size("tensor")
    tok_dev = resid.shape[1]
    d_model = resid.shape[2]
    group_tok = tok_dev * tensor_n
    used_n = used_adapters.shape[0]
    rank_n = gate_a.shape[2]
    feat_loc = gate_a.shape[1]
    slots_loc = gate_a.shape[0]
    hidden_local = gate_weight_matrix.shape[1]
    adapters_n = adapter_holder.shape[0]

    matches = used_adapters[:, None] == jnp.arange(adapters_n, dtype=jnp.int32)[None, :]
    slot_used = jnp.sum(jnp.where(matches, adapter_holder[None, :], 0), axis=1)
    picker = (slot_used[:, None] == jnp.arange(adapters_n, dtype=jnp.int32)[None, :]).astype(
        jnp.bfloat16
    )

    col_n = d_model // tensor_n
    col_first = lax.axis_index("tensor") * col_n
    db_block = lax.dynamic_slice_in_dim(down_b, col_first, col_n, 2)
    seq_n = lax.axis_size("seq")
    picker3 = picker.reshape(used_n, seq_n, slots_loc)

    def fetch(pieces, gather):
        widths = [p.shape[1] * p.shape[2] for p in pieces]
        pack = jnp.concatenate([p.reshape(slots_loc, -1) for p in pieces], axis=1)
        whole = gather(pack).reshape((seq_n,) + pack.shape)
        chosen = jnp.einsum(
            "ugs,gsx->ux", picker3, whole, preferred_element_type=jnp.float32
        ).astype(jnp.bfloat16)
        offs = [0]
        for w in widths:
            offs.append(offs[-1] + w)
        return [
            chosen[:, offs[i] : offs[i + 1]].reshape((used_n,) + pieces[i].shape[1:])
            for i in range(len(pieces))
        ]

    sel_ga, sel_ua, sel_db = fetch(
        (gate_a, up_a, db_block), lambda p: all_gather_rows(p, "seq", seq_n)
    )
    sel_gb, sel_ub, sel_da = fetch(
        (gate_b, up_b, down_a), lambda p: lax.all_gather(p, "seq", axis=0, tiled=False)
    )

    prompt_ends = jnp.cumsum(prompt_lengths[0])
    positions = jnp.arange(group_tok, dtype=jnp.int32)
    prompt_index = jnp.sum((positions[:, None] >= prompt_ends[None, :]).astype(jnp.int32), axis=1)
    prompts_n = prompt_lengths.shape[1]
    hits = prompt_index[:, None] == jnp.arange(prompts_n, dtype=jnp.int32)[None, :]
    tok_choice = jnp.sum(jnp.where(hits, prompt_choice[0][None, :], 0), axis=1)
    token_weights = (tok_choice[:, None] == jnp.arange(used_n, dtype=jnp.int32)[None, :]).astype(
        jnp.float32
    )
    row_first = lax.axis_index("tensor") * tok_dev
    own_weights = lax.dynamic_slice_in_dim(token_weights, row_first, tok_dev, 0)

    residual_float = resid[0].astype(jnp.float32)
    scale = lax.rsqrt(jnp.mean(residual_float * residual_float, axis=-1, keepdims=True) + 1e-06)
    normalized_input = (residual_float * scale * norm_gain.astype(jnp.float32)).astype(jnp.bfloat16)

    piece = all_gather_rows(normalized_input, "tensor", tensor_n)

    db_rows = sel_db.reshape(-1, d_model)
    db_all = lax.all_gather(db_rows, "tensor", axis=0, tiled=False).reshape(
        tensor_n, used_n * rank_n, col_n
    )

    def feat_major(a):
        return jnp.transpose(a, (1, 0, 2)).reshape(feat_loc, used_n * rank_n)

    both_in = jnp.concatenate([feat_major(sel_ga), feat_major(sel_ua)], axis=1)
    feat_first = lax.axis_index("tensor") * feat_loc
    own_cols = lax.dynamic_slice_in_dim(piece, feat_first, feat_loc, 1)
    low = jnp.dot(own_cols, both_in, preferred_element_type=jnp.float32).reshape(
        group_tok, 2, used_n, rank_n
    )
    partial_mid = jnp.sum(low * token_weights[:, None, :, None], axis=2)
    mids = all_reduce_sum(partial_mid, "tensor", tensor_n)
    mid_gate = mids[:, 0].astype(jnp.bfloat16)
    mid_up = mids[:, 1].astype(jnp.bfloat16)
    weights_bf = token_weights.astype(jnp.bfloat16)

    def spread(mid):
        return (mid[:, None, :] * weights_bf[:, :, None]).reshape(group_tok, used_n * rank_n)

    gate_part = jnp.dot(piece, gate_weight_matrix, preferred_element_type=jnp.float32)
    up_part = jnp.dot(piece, up_weight, preferred_element_type=jnp.float32)
    gate_adapter_rows = jnp.dot(
        spread(mid_gate),
        sel_gb.reshape(used_n * rank_n, hidden_local),
        preferred_element_type=jnp.float32,
    )
    up_adapter_rows = jnp.dot(
        spread(mid_up),
        sel_ub.reshape(used_n * rank_n, hidden_local),
        preferred_element_type=jnp.float32,
    )
    gate_preactivation = gate_part + adapter_scale * gate_adapter_rows
    up_preactivation = up_part + adapter_scale * up_adapter_rows
    hidden = (jax.nn.silu(gate_preactivation) * up_preactivation).astype(jnp.bfloat16)

    down_part = jnp.dot(hidden, w_down, preferred_element_type=jnp.float32).astype(jnp.bfloat16)
    da_cols = jnp.transpose(sel_da, (1, 0, 2)).reshape(hidden_local, used_n * rank_n)
    down_adapter_rows = jnp.dot(hidden, da_cols, preferred_element_type=jnp.float32).reshape(
        group_tok, used_n, rank_n
    )
    partial_down = select_token(down_adapter_rows, token_weights).astype(jnp.bfloat16)

    joined = jnp.concatenate([down_part, partial_down], axis=1)
    reduced = reduce_scatter_rows(joined, "tensor", tensor_n)
    down_total_sum = reduced[:, :d_model]
    mid_down = reduced[:, d_model:].astype(jnp.bfloat16)

    spread_down = (mid_down[:, None, :] * own_weights.astype(jnp.bfloat16)[:, :, None]).reshape(
        tok_dev, used_n * rank_n
    )
    adapter_down_term = jnp.einsum(
        "tk,jkc->tjc", spread_down, db_all, preferred_element_type=jnp.float32
    ).reshape(tok_dev, d_model)
    return (residual_float + down_total_sum + adapter_scale * adapter_down_term).astype(
        jnp.bfloat16
    )[None]


def solution(mesh):
    placed = (
        P("seq", "tensor", None),
        P(),
        P(None, "tensor"),
        P(None, "tensor"),
        P("tensor", None),
        P("seq", "tensor", None),
        P("seq", None, "tensor"),
        P("seq", "tensor", None),
        P("seq", None, "tensor"),
        P("seq", "tensor", None),
        P("seq", None, None),
        P("seq", None),
        P("seq", None),
        P(),
        P(),
    )
    return jax.shard_map(
        local, mesh=mesh, in_specs=placed, out_specs=P("seq", "tensor", None), check_vma=False
    )
```

```python
import jax
import jax.numpy as jnp
from jax import lax
from jax.sharding import PartitionSpec as P

adapter_scale = 0.5


def pick_rows(picker, stacked):
    flat = stacked.reshape(stacked.shape[0], -1)
    chosen = jnp.dot(picker, flat, preferred_element_type=jnp.float32).astype(jnp.bfloat16)
    return chosen.reshape((picker.shape[0],) + stacked.shape[1:])


def select_token(values, weights):
    return jnp.sum(values * weights[:, :, None], axis=1)


def exchange_levels(bits):
    if bits % 2 == 1:
        return [(0, 1)] + [(s, 2) for s in range(1, bits, 2)]
    return [(s, 1) for s in range(bits)]


def group_perm(axis_n, shift, size, d):
    return [
        (i, i + ((((i >> shift) + d) % size - (i >> shift) % size) << shift)) for i in range(axis_n)
    ]


def reduce_scatter_rows(x, axis_name, axis_n):
    bits = axis_n.bit_length() - 1
    me = lax.axis_index(axis_name)
    rows = x.shape[0] // axis_n
    acc = x.astype(jnp.float32).reshape((2,) * bits + (rows,) + x.shape[1:])
    left = bits
    for shift, nb in exchange_levels(bits):
        size = 1 << nb
        ax = left - nb
        acc = acc.reshape((2,) * ax + (size,) + acc.shape[left:])
        mine = (me >> shift) % size
        total = lax.dynamic_index_in_dim(acc, mine, axis=ax, keepdims=False)
        for d in range(1, size):
            send = lax.dynamic_index_in_dim(acc, (mine + d) % size, axis=ax, keepdims=False)
            got = lax.ppermute(
                send.astype(jnp.bfloat16), axis_name, group_perm(axis_n, shift, size, d)
            )
            total = total + got.astype(jnp.float32)
        acc = total
        left = ax
    return acc


def all_gather_rows(x, axis_name, axis_n):
    bits = axis_n.bit_length() - 1
    me = lax.axis_index(axis_name)
    acc = x
    for k, (shift, nb) in enumerate(reversed(exchange_levels(bits))):
        size = 1 << nb
        mine = (me >> shift) % size
        got = [acc] + [
            lax.ppermute(acc, axis_name, group_perm(axis_n, shift, size, d)) for d in range(1, size)
        ]
        blocks = []
        for q in range(size):
            dist = (mine - q) % size
            block = got[size - 1]
            for d in range(size - 2, -1, -1):
                block = jnp.where(dist == d, got[d], block)
            blocks.append(block)
        acc = jnp.stack(blocks, axis=k)
    return acc.reshape((axis_n * x.shape[0],) + x.shape[1:])


def all_reduce_sum(x, axis_name, axis_n):
    bits = axis_n.bit_length() - 1
    acc = x
    for shift, nb in exchange_levels(bits):
        size = 1 << nb
        total = acc
        for d in range(1, size):
            total = total + lax.ppermute(acc, axis_name, group_perm(axis_n, shift, size, d))
        acc = total
    return acc


def local(
    resid,
    norm_gain,
    gate_weight_matrix,
    up_weight,
    w_down,
    gate_a,
    gate_b,
    up_a,
    up_b,
    down_a,
    down_b,
    prompt_lengths,
    prompt_choice,
    used_adapters,
    adapter_holder,
):
    tensor_n = lax.axis_size("tensor")
    tok_dev = resid.shape[1]
    d_model = resid.shape[2]
    group_tok = tok_dev * tensor_n
    used_n = used_adapters.shape[0]
    rank_n = gate_a.shape[2]
    feat_loc = gate_a.shape[1]
    slots_loc = gate_a.shape[0]
    hidden_local = gate_weight_matrix.shape[1]
    adapters_n = adapter_holder.shape[0]

    matches = used_adapters[:, None] == jnp.arange(adapters_n, dtype=jnp.int32)[None, :]
    slot_used = jnp.sum(jnp.where(matches, adapter_holder[None, :], 0), axis=1)
    picker = (slot_used[:, None] == jnp.arange(adapters_n, dtype=jnp.int32)[None, :]).astype(
        jnp.bfloat16
    )

    col_n = d_model // tensor_n
    col_first = lax.axis_index("tensor") * col_n
    db_block = lax.dynamic_slice_in_dim(down_b, col_first, col_n, 2)
    seq_n = lax.axis_size("seq")
    picker3 = picker.reshape(used_n, seq_n, slots_loc)

    def fetch(pieces, gather):
        widths = [p.shape[1] * p.shape[2] for p in pieces]
        pack = jnp.concatenate([p.reshape(slots_loc, -1) for p in pieces], axis=1)
        whole = gather(pack).reshape((seq_n,) + pack.shape)
        chosen = jnp.einsum(
            "ugs,gsx->ux", picker3, whole, preferred_element_type=jnp.float32
        ).astype(jnp.bfloat16)
        offs = [0]
        for w in widths:
            offs.append(offs[-1] + w)
        return [
            chosen[:, offs[i] : offs[i + 1]].reshape((used_n,) + pieces[i].shape[1:])
            for i in range(len(pieces))
        ]

    sel_ga, sel_ua, sel_db = fetch(
        (gate_a, up_a, db_block), lambda p: all_gather_rows(p, "seq", seq_n)
    )
    sel_gb, sel_ub, sel_da = fetch(
        (gate_b, up_b, down_a), lambda p: lax.all_gather(p, "seq", axis=0, tiled=False)
    )

    prompt_ends = jnp.cumsum(prompt_lengths[0])
    positions = jnp.arange(group_tok, dtype=jnp.int32)
    prompt_index = jnp.sum((positions[:, None] >= prompt_ends[None, :]).astype(jnp.int32), axis=1)
    prompts_n = prompt_lengths.shape[1]
    hits = prompt_index[:, None] == jnp.arange(prompts_n, dtype=jnp.int32)[None, :]
    tok_choice = jnp.sum(jnp.where(hits, prompt_choice[0][None, :], 0), axis=1)
    token_weights = (tok_choice[:, None] == jnp.arange(used_n, dtype=jnp.int32)[None, :]).astype(
        jnp.float32
    )
    row_first = lax.axis_index("tensor") * tok_dev
    own_weights = lax.dynamic_slice_in_dim(token_weights, row_first, tok_dev, 0)

    residual_float = resid[0].astype(jnp.float32)
    scale = lax.rsqrt(jnp.mean(residual_float * residual_float, axis=-1, keepdims=True) + 1e-06)
    normalized_input = (residual_float * scale * norm_gain.astype(jnp.float32)).astype(jnp.bfloat16)

    piece = all_gather_rows(normalized_input, "tensor", tensor_n)

    db_rows = sel_db.reshape(-1, d_model)
    db_all = lax.all_gather(db_rows, "tensor", axis=0, tiled=False).reshape(
        tensor_n, used_n * rank_n, col_n
    )

    def feat_major(a):
        return jnp.transpose(a, (1, 0, 2)).reshape(feat_loc, used_n * rank_n)

    both_in = jnp.concatenate([feat_major(sel_ga), feat_major(sel_ua)], axis=1)
    feat_first = lax.axis_index("tensor") * feat_loc
    own_cols = lax.dynamic_slice_in_dim(piece, feat_first, feat_loc, 1)
    low = jnp.dot(own_cols, both_in, preferred_element_type=jnp.float32).reshape(
        group_tok, 2, used_n, rank_n
    )
    partial_mid = jnp.sum(low * token_weights[:, None, :, None], axis=2)
    mids = all_reduce_sum(partial_mid, "tensor", tensor_n)
    mid_gate = mids[:, 0].astype(jnp.bfloat16)
    mid_up = mids[:, 1].astype(jnp.bfloat16)
    weights_bf = token_weights.astype(jnp.bfloat16)

    def spread(mid):
        return (mid[:, None, :] * weights_bf[:, :, None]).reshape(group_tok, used_n * rank_n)

    gate_part = jnp.dot(piece, gate_weight_matrix, preferred_element_type=jnp.float32)
    up_part = jnp.dot(piece, up_weight, preferred_element_type=jnp.float32)
    gate_adapter_rows = jnp.dot(
        spread(mid_gate),
        sel_gb.reshape(used_n * rank_n, hidden_local),
        preferred_element_type=jnp.float32,
    )
    up_adapter_rows = jnp.dot(
        spread(mid_up),
        sel_ub.reshape(used_n * rank_n, hidden_local),
        preferred_element_type=jnp.float32,
    )
    gate_preactivation = gate_part + adapter_scale * gate_adapter_rows
    up_preactivation = up_part + adapter_scale * up_adapter_rows
    hidden = (jax.nn.silu(gate_preactivation) * up_preactivation).astype(jnp.bfloat16)

    down_part = jnp.dot(hidden, w_down, preferred_element_type=jnp.float32).astype(jnp.bfloat16)
    da_cols = jnp.transpose(sel_da, (1, 0, 2)).reshape(hidden_local, used_n * rank_n)
    down_adapter_rows = jnp.dot(hidden, da_cols, preferred_element_type=jnp.float32).reshape(
        group_tok, used_n, rank_n
    )
    partial_down = select_token(down_adapter_rows, token_weights).astype(jnp.bfloat16)

    joined = jnp.concatenate([down_part, partial_down], axis=1)
    reduced = reduce_scatter_rows(joined, "tensor", tensor_n)
    down_total_sum = reduced[:, :d_model]
    mid_down = reduced[:, d_model:].astype(jnp.bfloat16)

    spread_down = (mid_down[:, None, :] * own_weights.astype(jnp.bfloat16)[:, :, None]).reshape(
        tok_dev, used_n * rank_n
    )
    adapter_down_term = jnp.einsum(
        "tk,jkc->tjc", spread_down, db_all, preferred_element_type=jnp.float32
    ).reshape(tok_dev, d_model)
    return (residual_float + down_total_sum + adapter_scale * adapter_down_term).astype(
        jnp.bfloat16
    )[None]


def solution(mesh):
    placed = (
        P("seq", "tensor", None),
        P(),
        P(None, "tensor"),
        P(None, "tensor"),
        P("tensor", None),
        P("seq", "tensor", None),
        P("seq", None, "tensor"),
        P("seq", "tensor", None),
        P("seq", None, "tensor"),
        P("seq", "tensor", None),
        P("seq", None, None),
        P("seq", None),
        P("seq", None),
        P(),
        P(),
    )
    return jax.shard_map(
        local, mesh=mesh, in_specs=placed, out_specs=P("seq", "tensor", None), check_vma=False
    )
```

```python
import jax
import jax.numpy as jnp
from jax import lax
from jax.sharding import PartitionSpec as P

adapter_scale = 0.5


def pick_rows(picker, stacked):
    flat = stacked.reshape(stacked.shape[0], -1)
    chosen = jnp.dot(picker, flat, preferred_element_type=jnp.float32).astype(jnp.bfloat16)
    return chosen.reshape((picker.shape[0],) + stacked.shape[1:])


def select_token(values, weights):
    return jnp.sum(values * weights[:, :, None], axis=1)


def exchange_levels(bits):
    if bits % 2 == 1:
        return [(0, 1)] + [(s, 2) for s in range(1, bits, 2)]
    return [(s, 1) for s in range(bits)]


def group_perm(axis_n, shift, size, d):
    return [
        (i, i + ((((i >> shift) + d) % size - (i >> shift) % size) << shift)) for i in range(axis_n)
    ]


def reduce_scatter_rows(x, axis_name, axis_n):
    bits = axis_n.bit_length() - 1
    me = lax.axis_index(axis_name)
    rows = x.shape[0] // axis_n
    acc = x.astype(jnp.float32).reshape((2,) * bits + (rows,) + x.shape[1:])
    left = bits
    for shift, nb in exchange_levels(bits):
        size = 1 << nb
        ax = left - nb
        acc = acc.reshape((2,) * ax + (size,) + acc.shape[left:])
        mine = (me >> shift) % size
        total = lax.dynamic_index_in_dim(acc, mine, axis=ax, keepdims=False)
        for d in range(1, size):
            send = lax.dynamic_index_in_dim(acc, (mine + d) % size, axis=ax, keepdims=False)
            got = lax.ppermute(
                send.astype(jnp.bfloat16), axis_name, group_perm(axis_n, shift, size, d)
            )
            total = total + got.astype(jnp.float32)
        acc = total
        left = ax
    return acc


def all_gather_rows(x, axis_name, axis_n):
    bits = axis_n.bit_length() - 1
    me = lax.axis_index(axis_name)
    acc = x
    for k, (shift, nb) in enumerate(reversed(exchange_levels(bits))):
        size = 1 << nb
        mine = (me >> shift) % size
        got = [acc] + [
            lax.ppermute(acc, axis_name, group_perm(axis_n, shift, size, d)) for d in range(1, size)
        ]
        blocks = []
        for q in range(size):
            dist = (mine - q) % size
            block = got[size - 1]
            for d in range(size - 2, -1, -1):
                block = jnp.where(dist == d, got[d], block)
            blocks.append(block)
        acc = jnp.stack(blocks, axis=k)
    return acc.reshape((axis_n * x.shape[0],) + x.shape[1:])


def all_reduce_sum(x, axis_name, axis_n):
    bits = axis_n.bit_length() - 1
    acc = x
    for shift, nb in exchange_levels(bits):
        size = 1 << nb
        wire = acc.astype(jnp.bfloat16)
        total = acc
        for d in range(1, size):
            got = lax.ppermute(wire, axis_name, group_perm(axis_n, shift, size, d))
            total = total + got.astype(jnp.float32)
        acc = total
    return acc


def local(
    resid,
    norm_gain,
    gate_weight_matrix,
    up_weight,
    w_down,
    gate_a,
    gate_b,
    up_a,
    up_b,
    down_a,
    down_b,
    prompt_lengths,
    prompt_choice,
    used_adapters,
    adapter_holder,
):
    tensor_n = lax.axis_size("tensor")
    tok_dev = resid.shape[1]
    d_model = resid.shape[2]
    group_tok = tok_dev * tensor_n
    used_n = used_adapters.shape[0]
    rank_n = gate_a.shape[2]
    feat_loc = gate_a.shape[1]
    slots_loc = gate_a.shape[0]
    hidden_local = gate_weight_matrix.shape[1]
    adapters_n = adapter_holder.shape[0]

    matches = used_adapters[:, None] == jnp.arange(adapters_n, dtype=jnp.int32)[None, :]
    slot_used = jnp.sum(jnp.where(matches, adapter_holder[None, :], 0), axis=1)
    picker = (slot_used[:, None] == jnp.arange(adapters_n, dtype=jnp.int32)[None, :]).astype(
        jnp.bfloat16
    )

    col_n = d_model // tensor_n
    col_first = lax.axis_index("tensor") * col_n
    db_block = lax.dynamic_slice_in_dim(down_b, col_first, col_n, 2)
    seq_n = lax.axis_size("seq")
    picker3 = picker.reshape(used_n, seq_n, slots_loc)

    def fetch(pieces, gather):
        widths = [p.shape[1] * p.shape[2] for p in pieces]
        pack = jnp.concatenate([p.reshape(slots_loc, -1) for p in pieces], axis=1)
        whole = gather(pack).reshape((seq_n,) + pack.shape)
        chosen = jnp.einsum(
            "ugs,gsx->ux", picker3, whole, preferred_element_type=jnp.float32
        ).astype(jnp.bfloat16)
        offs = [0]
        for w in widths:
            offs.append(offs[-1] + w)
        return [
            chosen[:, offs[i] : offs[i + 1]].reshape((used_n,) + pieces[i].shape[1:])
            for i in range(len(pieces))
        ]

    sel_ga, sel_ua, sel_db = fetch(
        (gate_a, up_a, db_block), lambda p: all_gather_rows(p, "seq", seq_n)
    )
    sel_gb, sel_ub, sel_da = fetch(
        (gate_b, up_b, down_a), lambda p: lax.all_gather(p, "seq", axis=0, tiled=False)
    )

    prompt_ends = jnp.cumsum(prompt_lengths[0])
    positions = jnp.arange(group_tok, dtype=jnp.int32)
    prompt_index = jnp.sum((positions[:, None] >= prompt_ends[None, :]).astype(jnp.int32), axis=1)
    prompts_n = prompt_lengths.shape[1]
    hits = prompt_index[:, None] == jnp.arange(prompts_n, dtype=jnp.int32)[None, :]
    tok_choice = jnp.sum(jnp.where(hits, prompt_choice[0][None, :], 0), axis=1)
    token_weights = (tok_choice[:, None] == jnp.arange(used_n, dtype=jnp.int32)[None, :]).astype(
        jnp.float32
    )
    row_first = lax.axis_index("tensor") * tok_dev
    own_weights = lax.dynamic_slice_in_dim(token_weights, row_first, tok_dev, 0)

    residual_float = resid[0].astype(jnp.float32)
    scale = lax.rsqrt(jnp.mean(residual_float * residual_float, axis=-1, keepdims=True) + 1e-06)
    normalized_input = (residual_float * scale * norm_gain.astype(jnp.float32)).astype(jnp.bfloat16)

    piece = all_gather_rows(normalized_input, "tensor", tensor_n)

    db_rows = sel_db.reshape(-1, d_model)
    db_all = lax.all_gather(db_rows, "tensor", axis=0, tiled=False).reshape(
        tensor_n, used_n * rank_n, col_n
    )

    def feat_major(a):
        return jnp.transpose(a, (1, 0, 2)).reshape(feat_loc, used_n * rank_n)

    both_in = jnp.concatenate([feat_major(sel_ga), feat_major(sel_ua)], axis=1)
    feat_first = lax.axis_index("tensor") * feat_loc
    own_cols = lax.dynamic_slice_in_dim(piece, feat_first, feat_loc, 1)
    low = jnp.dot(own_cols, both_in, preferred_element_type=jnp.float32).reshape(
        group_tok, 2, used_n, rank_n
    )
    partial_mid = jnp.sum(low * token_weights[:, None, :, None], axis=2)
    mids = all_reduce_sum(partial_mid, "tensor", tensor_n)
    mid_gate = mids[:, 0].astype(jnp.bfloat16)
    mid_up = mids[:, 1].astype(jnp.bfloat16)
    weights_bf = token_weights.astype(jnp.bfloat16)

    def spread(mid):
        return (mid[:, None, :] * weights_bf[:, :, None]).reshape(group_tok, used_n * rank_n)

    gate_part = jnp.dot(piece, gate_weight_matrix, preferred_element_type=jnp.float32)
    up_part = jnp.dot(piece, up_weight, preferred_element_type=jnp.float32)
    gate_adapter_rows = jnp.dot(
        spread(mid_gate),
        sel_gb.reshape(used_n * rank_n, hidden_local),
        preferred_element_type=jnp.float32,
    )
    up_adapter_rows = jnp.dot(
        spread(mid_up),
        sel_ub.reshape(used_n * rank_n, hidden_local),
        preferred_element_type=jnp.float32,
    )
    gate_preactivation = gate_part + adapter_scale * gate_adapter_rows
    up_preactivation = up_part + adapter_scale * up_adapter_rows
    hidden = (jax.nn.silu(gate_preactivation) * up_preactivation).astype(jnp.bfloat16)

    down_part = jnp.dot(hidden, w_down, preferred_element_type=jnp.float32).astype(jnp.bfloat16)
    da_cols = jnp.transpose(sel_da, (1, 0, 2)).reshape(hidden_local, used_n * rank_n)
    down_adapter_rows = jnp.dot(hidden, da_cols, preferred_element_type=jnp.float32).reshape(
        group_tok, used_n, rank_n
    )
    partial_down = select_token(down_adapter_rows, token_weights).astype(jnp.bfloat16)

    joined = jnp.concatenate([down_part, partial_down], axis=1)
    reduced = reduce_scatter_rows(joined, "tensor", tensor_n)
    down_total_sum = reduced[:, :d_model]
    mid_down = reduced[:, d_model:].astype(jnp.bfloat16)

    spread_down = (mid_down[:, None, :] * own_weights.astype(jnp.bfloat16)[:, :, None]).reshape(
        tok_dev, used_n * rank_n
    )
    adapter_down_term = jnp.einsum(
        "tk,jkc->tjc", spread_down, db_all, preferred_element_type=jnp.float32
    ).reshape(tok_dev, d_model)
    return (residual_float + down_total_sum + adapter_scale * adapter_down_term).astype(
        jnp.bfloat16
    )[None]


def solution(mesh):
    placed = (
        P("seq", "tensor", None),
        P(),
        P(None, "tensor"),
        P(None, "tensor"),
        P("tensor", None),
        P("seq", "tensor", None),
        P("seq", None, "tensor"),
        P("seq", "tensor", None),
        P("seq", None, "tensor"),
        P("seq", "tensor", None),
        P("seq", None, None),
        P("seq", None),
        P("seq", None),
        P(),
        P(),
    )
    return jax.shard_map(
        local, mesh=mesh, in_specs=placed, out_specs=P("seq", "tensor", None), check_vma=False
    )
```

```python
import jax
import jax.numpy as jnp
from jax import lax
from jax.sharding import PartitionSpec as P

adapter_scale = 0.5


def pick_rows(picker, stacked):
    flat = stacked.reshape(stacked.shape[0], -1)
    chosen = jnp.dot(picker, flat, preferred_element_type=jnp.float32).astype(jnp.bfloat16)
    return chosen.reshape((picker.shape[0],) + stacked.shape[1:])


def select_token(values, weights):
    return jnp.sum(values * weights[:, :, None], axis=1)


def exchange_levels(bits):
    if bits % 2 == 1:
        return [(0, 1)] + [(s, 2) for s in range(1, bits, 2)]
    return [(s, 2) for s in range(0, bits, 2)]


def group_perm(axis_n, shift, size, d):
    return [
        (i, i + ((((i >> shift) + d) % size - (i >> shift) % size) << shift)) for i in range(axis_n)
    ]


def reduce_scatter_rows(x, axis_name, axis_n):
    bits = axis_n.bit_length() - 1
    me = lax.axis_index(axis_name)
    rows = x.shape[0] // axis_n
    acc = x.astype(jnp.float32).reshape((2,) * bits + (rows,) + x.shape[1:])
    left = bits
    for shift, nb in exchange_levels(bits):
        size = 1 << nb
        ax = left - nb
        acc = acc.reshape((2,) * ax + (size,) + acc.shape[left:])
        mine = (me >> shift) % size
        total = lax.dynamic_index_in_dim(acc, mine, axis=ax, keepdims=False)
        for d in range(1, size):
            send = lax.dynamic_index_in_dim(acc, (mine + d) % size, axis=ax, keepdims=False)
            got = lax.ppermute(
                send.astype(jnp.bfloat16), axis_name, group_perm(axis_n, shift, size, d)
            )
            total = total + got.astype(jnp.float32)
        acc = total
        left = ax
    return acc


def all_gather_rows(x, axis_name, axis_n):
    bits = axis_n.bit_length() - 1
    me = lax.axis_index(axis_name)
    acc = x
    for k, (shift, nb) in enumerate(reversed(exchange_levels(bits))):
        size = 1 << nb
        mine = (me >> shift) % size
        got = [acc] + [
            lax.ppermute(acc, axis_name, group_perm(axis_n, shift, size, d)) for d in range(1, size)
        ]
        blocks = []
        for q in range(size):
            dist = (mine - q) % size
            block = got[size - 1]
            for d in range(size - 2, -1, -1):
                block = jnp.where(dist == d, got[d], block)
            blocks.append(block)
        acc = jnp.stack(blocks, axis=k)
    return acc.reshape((axis_n * x.shape[0],) + x.shape[1:])


def all_reduce_sum(x, axis_name, axis_n):
    bits = axis_n.bit_length() - 1
    acc = x
    for shift, nb in exchange_levels(bits):
        size = 1 << nb
        total = acc
        for d in range(1, size):
            total = total + lax.ppermute(acc, axis_name, group_perm(axis_n, shift, size, d))
        acc = total
    return acc


def local(
    resid,
    norm_gain,
    gate_weight_matrix,
    up_weight,
    w_down,
    gate_a,
    gate_b,
    up_a,
    up_b,
    down_a,
    down_b,
    prompt_lengths,
    prompt_choice,
    used_adapters,
    adapter_holder,
):
    tensor_n = lax.axis_size("tensor")
    tok_dev = resid.shape[1]
    d_model = resid.shape[2]
    group_tok = tok_dev * tensor_n
    used_n = used_adapters.shape[0]
    rank_n = gate_a.shape[2]
    feat_loc = gate_a.shape[1]
    slots_loc = gate_a.shape[0]
    hidden_local = gate_weight_matrix.shape[1]
    adapters_n = adapter_holder.shape[0]

    matches = used_adapters[:, None] == jnp.arange(adapters_n, dtype=jnp.int32)[None, :]
    slot_used = jnp.sum(jnp.where(matches, adapter_holder[None, :], 0), axis=1)
    picker = (slot_used[:, None] == jnp.arange(adapters_n, dtype=jnp.int32)[None, :]).astype(
        jnp.bfloat16
    )

    col_n = d_model // tensor_n
    col_first = lax.axis_index("tensor") * col_n
    db_block = lax.dynamic_slice_in_dim(down_b, col_first, col_n, 2)
    seq_n = lax.axis_size("seq")
    picker3 = picker.reshape(used_n, seq_n, slots_loc)

    def fetch(pieces, gather):
        widths = [p.shape[1] * p.shape[2] for p in pieces]
        pack = jnp.concatenate([p.reshape(slots_loc, -1) for p in pieces], axis=1)
        whole = gather(pack).reshape((seq_n,) + pack.shape)
        chosen = jnp.einsum(
            "ugs,gsx->ux", picker3, whole, preferred_element_type=jnp.float32
        ).astype(jnp.bfloat16)
        offs = [0]
        for w in widths:
            offs.append(offs[-1] + w)
        return [
            chosen[:, offs[i] : offs[i + 1]].reshape((used_n,) + pieces[i].shape[1:])
            for i in range(len(pieces))
        ]

    sel_ga, sel_ua, sel_db = fetch(
        (gate_a, up_a, db_block), lambda p: all_gather_rows(p, "seq", seq_n)
    )
    sel_gb, sel_ub, sel_da = fetch(
        (gate_b, up_b, down_a), lambda p: lax.all_gather(p, "seq", axis=0, tiled=False)
    )

    prompt_ends = jnp.cumsum(prompt_lengths[0])
    positions = jnp.arange(group_tok, dtype=jnp.int32)
    prompt_index = jnp.sum((positions[:, None] >= prompt_ends[None, :]).astype(jnp.int32), axis=1)
    prompts_n = prompt_lengths.shape[1]
    hits = prompt_index[:, None] == jnp.arange(prompts_n, dtype=jnp.int32)[None, :]
    tok_choice = jnp.sum(jnp.where(hits, prompt_choice[0][None, :], 0), axis=1)
    token_weights = (tok_choice[:, None] == jnp.arange(used_n, dtype=jnp.int32)[None, :]).astype(
        jnp.float32
    )
    row_first = lax.axis_index("tensor") * tok_dev
    own_weights = lax.dynamic_slice_in_dim(token_weights, row_first, tok_dev, 0)

    residual_float = resid[0].astype(jnp.float32)
    scale = lax.rsqrt(jnp.mean(residual_float * residual_float, axis=-1, keepdims=True) + 1e-06)
    normalized_input = (residual_float * scale * norm_gain.astype(jnp.float32)).astype(jnp.bfloat16)

    piece = all_gather_rows(normalized_input, "tensor", tensor_n)

    db_rows = sel_db.reshape(-1, d_model)
    db_all = lax.all_gather(db_rows, "tensor", axis=0, tiled=False).reshape(
        tensor_n, used_n * rank_n, col_n
    )

    def feat_major(a):
        return jnp.transpose(a, (1, 0, 2)).reshape(feat_loc, used_n * rank_n)

    both_in = jnp.concatenate([feat_major(sel_ga), feat_major(sel_ua)], axis=1)
    feat_first = lax.axis_index("tensor") * feat_loc
    own_cols = lax.dynamic_slice_in_dim(piece, feat_first, feat_loc, 1)
    low = jnp.dot(own_cols, both_in, preferred_element_type=jnp.float32).reshape(
        group_tok, 2, used_n, rank_n
    )
    partial_mid = jnp.sum(low * token_weights[:, None, :, None], axis=2)
    mids = all_reduce_sum(partial_mid, "tensor", tensor_n)
    mid_gate = mids[:, 0].astype(jnp.bfloat16)
    mid_up = mids[:, 1].astype(jnp.bfloat16)
    weights_bf = token_weights.astype(jnp.bfloat16)

    def spread(mid):
        return (mid[:, None, :] * weights_bf[:, :, None]).reshape(group_tok, used_n * rank_n)

    gate_part = jnp.dot(piece, gate_weight_matrix, preferred_element_type=jnp.float32)
    up_part = jnp.dot(piece, up_weight, preferred_element_type=jnp.float32)
    gate_adapter_rows = jnp.dot(
        spread(mid_gate),
        sel_gb.reshape(used_n * rank_n, hidden_local),
        preferred_element_type=jnp.float32,
    )
    up_adapter_rows = jnp.dot(
        spread(mid_up),
        sel_ub.reshape(used_n * rank_n, hidden_local),
        preferred_element_type=jnp.float32,
    )
    gate_preactivation = gate_part + adapter_scale * gate_adapter_rows
    up_preactivation = up_part + adapter_scale * up_adapter_rows
    hidden = (jax.nn.silu(gate_preactivation) * up_preactivation).astype(jnp.bfloat16)

    down_part = jnp.dot(hidden, w_down, preferred_element_type=jnp.float32).astype(jnp.bfloat16)
    da_cols = jnp.transpose(sel_da, (1, 0, 2)).reshape(hidden_local, used_n * rank_n)
    down_adapter_rows = jnp.dot(hidden, da_cols, preferred_element_type=jnp.float32).reshape(
        group_tok, used_n, rank_n
    )
    partial_down = select_token(down_adapter_rows, token_weights).astype(jnp.bfloat16)

    joined = jnp.concatenate([down_part, partial_down], axis=1)
    reduced = reduce_scatter_rows(joined, "tensor", tensor_n)
    down_total_sum = reduced[:, :d_model]
    mid_down = reduced[:, d_model:].astype(jnp.bfloat16)

    spread_down = (mid_down[:, None, :] * own_weights.astype(jnp.bfloat16)[:, :, None]).reshape(
        tok_dev, used_n * rank_n
    )
    adapter_down_term = jnp.einsum(
        "tk,jkc->tjc", spread_down, db_all, preferred_element_type=jnp.float32
    ).reshape(tok_dev, d_model)
    return (residual_float + down_total_sum + adapter_scale * adapter_down_term).astype(
        jnp.bfloat16
    )[None]


def solution(mesh):
    placed = (
        P("seq", "tensor", None),
        P(),
        P(None, "tensor"),
        P(None, "tensor"),
        P("tensor", None),
        P("seq", "tensor", None),
        P("seq", None, "tensor"),
        P("seq", "tensor", None),
        P("seq", None, "tensor"),
        P("seq", "tensor", None),
        P("seq", None, None),
        P("seq", None),
        P("seq", None),
        P(),
        P(),
    )
    return jax.shard_map(
        local, mesh=mesh, in_specs=placed, out_specs=P("seq", "tensor", None), check_vma=False
    )
```

```python
import jax
import jax.numpy as jnp
from jax import lax
from jax.sharding import PartitionSpec as P

adapter_scale = 0.5


def pick_rows(picker, stacked):
    flat = stacked.reshape(stacked.shape[0], -1)
    chosen = jnp.dot(picker, flat, preferred_element_type=jnp.float32).astype(jnp.bfloat16)
    return chosen.reshape((picker.shape[0],) + stacked.shape[1:])


def select_token(values, weights):
    return jnp.sum(values * weights[:, :, None], axis=1)


def exchange_levels(bits):
    if bits % 2 == 1:
        return [(0, 1)] + [(s, 2) for s in range(1, bits, 2)]
    return [(s, 1) for s in range(bits)]


def group_perm(axis_n, shift, size, d):
    return [
        (i, i + ((((i >> shift) + d) % size - (i >> shift) % size) << shift)) for i in range(axis_n)
    ]


def reduce_scatter_rows(x, axis_name, axis_n):
    bits = axis_n.bit_length() - 1
    me = lax.axis_index(axis_name)
    rows = x.shape[0] // axis_n
    acc = x.reshape((2,) * bits + (rows,) + x.shape[1:])
    left = bits
    for shift, nb in exchange_levels(bits):
        size = 1 << nb
        ax = left - nb
        acc = acc.reshape((2,) * ax + (size,) + acc.shape[left:])
        mine = (me >> shift) % size
        total = lax.dynamic_index_in_dim(acc, mine, axis=ax, keepdims=False).astype(jnp.float32)
        for d in range(1, size):
            send = lax.dynamic_index_in_dim(acc, (mine + d) % size, axis=ax, keepdims=False)
            got = lax.ppermute(
                send.astype(jnp.bfloat16), axis_name, group_perm(axis_n, shift, size, d)
            )
            total = total + got.astype(jnp.float32)
        acc = total
        left = ax
    return acc


def all_gather_rows(x, axis_name, axis_n):
    bits = axis_n.bit_length() - 1
    me = lax.axis_index(axis_name)
    acc = x
    for k, (shift, nb) in enumerate(reversed(exchange_levels(bits))):
        size = 1 << nb
        mine = (me >> shift) % size
        got = [acc] + [
            lax.ppermute(acc, axis_name, group_perm(axis_n, shift, size, d)) for d in range(1, size)
        ]
        blocks = []
        for q in range(size):
            dist = (mine - q) % size
            block = got[size - 1]
            for d in range(size - 2, -1, -1):
                block = jnp.where(dist == d, got[d], block)
            blocks.append(block)
        acc = jnp.stack(blocks, axis=k)
    return acc.reshape((axis_n * x.shape[0],) + x.shape[1:])


def all_reduce_sum(x, axis_name, axis_n):
    bits = axis_n.bit_length() - 1
    acc = x
    for shift, nb in exchange_levels(bits):
        size = 1 << nb
        total = acc
        for d in range(1, size):
            total = total + lax.ppermute(acc, axis_name, group_perm(axis_n, shift, size, d))
        acc = total
    return acc


def local(
    resid,
    norm_gain,
    gate_weight_matrix,
    up_weight,
    w_down,
    gate_a,
    gate_b,
    up_a,
    up_b,
    down_a,
    down_b,
    prompt_lengths,
    prompt_choice,
    used_adapters,
    adapter_holder,
):
    tensor_n = lax.axis_size("tensor")
    tok_dev = resid.shape[1]
    d_model = resid.shape[2]
    group_tok = tok_dev * tensor_n
    used_n = used_adapters.shape[0]
    rank_n = gate_a.shape[2]
    feat_loc = gate_a.shape[1]
    slots_loc = gate_a.shape[0]
    hidden_local = gate_weight_matrix.shape[1]
    adapters_n = adapter_holder.shape[0]

    matches = used_adapters[:, None] == jnp.arange(adapters_n, dtype=jnp.int32)[None, :]
    slot_used = jnp.sum(jnp.where(matches, adapter_holder[None, :], 0), axis=1)
    picker = (slot_used[:, None] == jnp.arange(adapters_n, dtype=jnp.int32)[None, :]).astype(
        jnp.bfloat16
    )

    col_n = d_model // tensor_n
    col_first = lax.axis_index("tensor") * col_n
    db_block = lax.dynamic_slice_in_dim(down_b, col_first, col_n, 2)
    seq_n = lax.axis_size("seq")
    picker3 = picker.reshape(used_n, seq_n, slots_loc)

    def fetch(pieces, gather):
        widths = [p.shape[1] * p.shape[2] for p in pieces]
        pack = jnp.concatenate([p.reshape(slots_loc, -1) for p in pieces], axis=1)
        whole = gather(pack).reshape((seq_n,) + pack.shape)
        chosen = jnp.einsum(
            "ugs,gsx->ux", picker3, whole, preferred_element_type=jnp.float32
        ).astype(jnp.bfloat16)
        offs = [0]
        for w in widths:
            offs.append(offs[-1] + w)
        return [
            chosen[:, offs[i] : offs[i + 1]].reshape((used_n,) + pieces[i].shape[1:])
            for i in range(len(pieces))
        ]

    sel_ga, sel_ua, sel_db = fetch(
        (gate_a, up_a, db_block), lambda p: all_gather_rows(p, "seq", seq_n)
    )
    sel_gb, sel_ub, sel_da = fetch(
        (gate_b, up_b, down_a), lambda p: lax.all_gather(p, "seq", axis=0, tiled=False)
    )

    prompt_ends = jnp.cumsum(prompt_lengths[0])
    positions = jnp.arange(group_tok, dtype=jnp.int32)
    prompt_index = jnp.sum((positions[:, None] >= prompt_ends[None, :]).astype(jnp.int32), axis=1)
    prompts_n = prompt_lengths.shape[1]
    hits = prompt_index[:, None] == jnp.arange(prompts_n, dtype=jnp.int32)[None, :]
    tok_choice = jnp.sum(jnp.where(hits, prompt_choice[0][None, :], 0), axis=1)
    token_weights = (tok_choice[:, None] == jnp.arange(used_n, dtype=jnp.int32)[None, :]).astype(
        jnp.float32
    )
    row_first = lax.axis_index("tensor") * tok_dev
    own_weights = lax.dynamic_slice_in_dim(token_weights, row_first, tok_dev, 0)

    residual_float = resid[0].astype(jnp.float32)
    scale = lax.rsqrt(jnp.mean(residual_float * residual_float, axis=-1, keepdims=True) + 1e-06)
    normalized_input = (residual_float * scale * norm_gain.astype(jnp.float32)).astype(jnp.bfloat16)

    piece = all_gather_rows(normalized_input, "tensor", tensor_n)

    db_rows = sel_db.reshape(-1, d_model)
    db_all = lax.all_gather(db_rows, "tensor", axis=0, tiled=False).reshape(
        tensor_n, used_n * rank_n, col_n
    )

    def feat_major(a):
        return jnp.transpose(a, (1, 0, 2)).reshape(feat_loc, used_n * rank_n)

    both_in = jnp.concatenate([feat_major(sel_ga), feat_major(sel_ua)], axis=1)
    feat_first = lax.axis_index("tensor") * feat_loc
    own_cols = lax.dynamic_slice_in_dim(piece, feat_first, feat_loc, 1)
    low = jnp.dot(own_cols, both_in, preferred_element_type=jnp.float32).reshape(
        group_tok, 2, used_n, rank_n
    )
    partial_mid = jnp.sum(low * token_weights[:, None, :, None], axis=2)
    mids = all_reduce_sum(partial_mid, "tensor", tensor_n)
    mid_gate = mids[:, 0].astype(jnp.bfloat16)
    mid_up = mids[:, 1].astype(jnp.bfloat16)
    weights_bf = token_weights.astype(jnp.bfloat16)

    def spread(mid):
        return (mid[:, None, :] * weights_bf[:, :, None]).reshape(group_tok, used_n * rank_n)

    gate_part = jnp.dot(piece, gate_weight_matrix, preferred_element_type=jnp.float32)
    up_part = jnp.dot(piece, up_weight, preferred_element_type=jnp.float32)
    gate_adapter_rows = jnp.dot(
        spread(mid_gate),
        sel_gb.reshape(used_n * rank_n, hidden_local),
        preferred_element_type=jnp.float32,
    )
    up_adapter_rows = jnp.dot(
        spread(mid_up),
        sel_ub.reshape(used_n * rank_n, hidden_local),
        preferred_element_type=jnp.float32,
    )
    gate_preactivation = gate_part + adapter_scale * gate_adapter_rows
    up_preactivation = up_part + adapter_scale * up_adapter_rows
    hidden = (jax.nn.silu(gate_preactivation) * up_preactivation).astype(jnp.bfloat16)

    down_part = jnp.dot(hidden, w_down, preferred_element_type=jnp.float32).astype(jnp.bfloat16)
    da_cols = jnp.transpose(sel_da, (1, 0, 2)).reshape(hidden_local, used_n * rank_n)
    down_adapter_rows = jnp.dot(hidden, da_cols, preferred_element_type=jnp.float32).reshape(
        group_tok, used_n, rank_n
    )
    partial_down = select_token(down_adapter_rows, token_weights).astype(jnp.bfloat16)

    joined = jnp.concatenate([down_part, partial_down], axis=1)
    reduced = reduce_scatter_rows(joined, "tensor", tensor_n)
    down_total_sum = reduced[:, :d_model]
    mid_down = reduced[:, d_model:].astype(jnp.bfloat16)

    spread_down = (mid_down[:, None, :] * own_weights.astype(jnp.bfloat16)[:, :, None]).reshape(
        tok_dev, used_n * rank_n
    )
    adapter_down_term = jnp.einsum(
        "tk,jkc->tjc", spread_down, db_all, preferred_element_type=jnp.float32
    ).reshape(tok_dev, d_model)
    return (residual_float + down_total_sum + adapter_scale * adapter_down_term).astype(
        jnp.bfloat16
    )[None]


def solution(mesh):
    placed = (
        P("seq", "tensor", None),
        P(),
        P(None, "tensor"),
        P(None, "tensor"),
        P("tensor", None),
        P("seq", "tensor", None),
        P("seq", None, "tensor"),
        P("seq", "tensor", None),
        P("seq", None, "tensor"),
        P("seq", "tensor", None),
        P("seq", None, None),
        P("seq", None),
        P("seq", None),
        P(),
        P(),
    )
    return jax.shard_map(
        local, mesh=mesh, in_specs=placed, out_specs=P("seq", "tensor", None), check_vma=False
    )
```
